32 devices in a mesh: grp: 1, seq: 4 (over z), dp: 4 (over y, x), head: 2 (over core).
Axes of the slice: x: 2, y: 2, z: 4, core: 2. Of those that a mesh axis runs over, the one named last changes fastest.
Arguments:
- tokens_in: bfloat16 [4, 1024, 4096], P(('grp', 'dp'), 'seq'), may hold values from -6 to 6
- positions: int32 [4, 1024], P(('grp', 'dp'), 'seq'), may hold values from 0 to 1023, as said below
- doc_start: int32 [4, 1024], P(('grp', 'dp'), 'seq'), may hold values from 0 to 1, as said below
- feature_weight: bfloat16 [4096, 4096], P(('seq', 'dp'), 'head'), may hold values from -0.09375 to 0.09375
- state_weight: bfloat16 [4096, 128], P(('seq', 'dp')), may hold values from -0.01171875 to 0.01171875
- step_weight: bfloat16 [4096, 32], P(('seq', 'dp'), 'head'), may hold values from -0.09375 to 0.09375
- step_bias: float32 [32], P('head'), may hold values from -1 to 0.5
- decay_log: float32 [32], P('head')
- skip_gain: float32 [32], P('head'), may hold values from 0.4 to 1.9
- norm_gain: float32 [4096], P('head'), may hold values from 0.5 to 1.5
Outputs:
- mixed: bfloat16 [4, 1024, 4096], P(('grp', 'dp'), 'seq', 'head')
The draws below stay inside these ranges and needn't reach their ends.
Inputs may be any that keep to these rules, and one draw needn't show every extreme that they name: Each sequence's rows carry every position once. Cut each device's 256 rows into 4 equal slots in order: the positions of slot k all lie in [k * 256, (k + 1) * 256). `doc_start`: position 0 of every sequence holds 1; a sequence holds at most 4 ones.
All inputs are finite; a program needn't handle non-finite values.
Results may differ from the reference program's by a relative error of at most 0.0062.
Values may be sent and summed in bfloat16 or wider, within the bound.
No kernel may reach another device: no remote copies, remote signals or barrier semaphores. Data moves between devices by JAX's collectives and lax.ppermute only.
A program may use at most 128 MiB of HBM per device.

```python
import jax
import jax.numpy as jnp
from jax import lax

D = 4096
H = 32
P_SIZE = 128
N = 64
TOK_DEV = 256
L = 1024
SEQS = 4


def draw_positions(key, part):
    shards = L // TOK_DEV
    slot_rows = TOK_DEV // shards
    keys = jax.random.split(key, SEQS * shards)
    orders = jax.vmap(lambda single: jax.random.permutation(single, TOK_DEV))(keys).astype(jnp.int32)
    orders = orders.reshape(SEQS, shards, TOK_DEV)
    orders = orders + (jnp.arange(shards, dtype=jnp.int32) * TOK_DEV)[None, :, None]
    orders = orders.reshape(SEQS, shards, shards, slot_rows).transpose(0, 2, 1, 3)
    return orders.reshape(SEQS, L).astype(jnp.int32)


def draw_doc_start(key, part):
    cuts = jax.random.randint(key, (SEQS, 3), 1, L)
    places = jnp.arange(L, dtype=jnp.int32)
    marked = jnp.any(places[None, None, :] == cuts[:, :, None], axis=1) | (places[None, :] == 0)
    return marked.astype(jnp.int32)


def draw_decay_log(key, part):
    first, second, third = jax.random.split(key, 3)
    ranks = jax.random.permutation(first, H)
    quick = ranks < H // 2
    quick_rate = jnp.exp(jax.random.uniform(second, (H,), jnp.float32, jnp.log(0.015), jnp.log(0.05)))
    slow_rate = jnp.exp(jax.random.uniform(third, (H,), jnp.float32, jnp.log(0.1), jnp.log(1.5))) / L
    return jnp.log(jnp.where(quick, quick_rate, slow_rate)).astype(jnp.float32)


def draw_skip_gain(key, part):
    ramp = jnp.arange(H, dtype=jnp.float32) / max(H - 1, 1)
    spread = jnp.clip(0.1 * jax.random.normal(key, (H,), jnp.float32), -0.2, 0.2)
    return (0.5 * jnp.power(3.0, ramp) * jnp.exp(spread)).astype(jnp.float32)


def block_levels(key, extent, cuts, low, top_value):
    def one(axis_at, parts):
        heights = jax.random.uniform(jax.random.fold_in(jax.random.fold_in(key, 6), axis_at), (parts,), jnp.float32, low / len(cuts), top_value / len(cuts))
        return jnp.repeat(jnp.exp(heights), extent[axis_at] // parts).reshape((-1,) + (1,) * (len(extent) - axis_at - 1))

    loudness = one(*cuts[0])
    for cut in cuts[1:]:
        loudness = loudness * one(*cut)
    return loudness


def normal_values(own_key, extent, deviation, limit, cuts=(), kind=jnp.bfloat16):
    values = deviation * jax.random.normal(own_key, extent, jnp.float32)
    if cuts:
        values = values * block_levels(own_key, extent, cuts, -0.22, 0.18)
    return jnp.clip(values, -limit, limit).astype(kind)


def setup_inputs(seed: int = 0, part: int = 0) -> dict:
    streams_of = jax.random.split(jax.random.key(seed), 11)
    part_keys = jax.random.split(jax.random.fold_in(streams_of[10], part), 11)
    return {
        "tokens_in": normal_values(part_keys[0], (SEQS, L, D), 1.0, 6.0, ((0, 4), (1, 4))),
        "positions": draw_positions(jax.random.fold_in(jax.random.fold_in(streams_of[10], part), 71), part),
        "doc_start": draw_doc_start(jax.random.fold_in(jax.random.fold_in(streams_of[10], part), 71), part),
        "feature_weight": normal_values(streams_of[3], (D, H * P_SIZE), D ** -0.5, 0.09375, ((0, 16), (1, 2))),
        "state_weight": normal_values(streams_of[4], (D, 2 * N), (D * N) ** -0.5, 0.01171875, ((0, 16),)),
        "step_weight": normal_values(streams_of[5], (D, H), D ** -0.5, 0.09375, ((0, 16), (1, 2))),
        "step_bias": jnp.clip(-1.0 + 1.5 * jax.random.uniform(streams_of[6], (H,), jnp.float32) ** block_levels(streams_of[6], (H,), ((0, 2),), -0.2, 0.2), -1.0, 0.5),
        "decay_log": draw_decay_log(jax.random.fold_in(streams_of[10], 71), part),
        "skip_gain": draw_skip_gain(jax.random.fold_in(streams_of[10], 71), part),
        "norm_gain": jnp.clip(1.0 + 0.1 * jax.random.normal(streams_of[9], (H * P_SIZE,), jnp.float32), 0.5, 1.5),
    }


def head_terms(inputs, scores, same_doc, doc_index, b_float):
    cum_head, step_head, x_head = inputs
    decay = jnp.exp(-jnp.abs(cum_head[:, None] - cum_head[None, :])) * same_doc
    mixing = scores * decay * step_head[None, :]
    x_float = x_head.astype(jnp.float32)
    y_local = jnp.dot(mixing, x_float, precision=lax.Precision.HIGHEST)
    end_weight = jnp.exp(cum_head[-1] - cum_head) * (doc_index == doc_index[-1]) * step_head
    begin_weight = jnp.exp(cum_head) * (doc_index == 0) * step_head
    state_end = jnp.dot((b_float * end_weight[:, None]).T, x_float, precision=lax.Precision.HIGHEST)
    state_begin = jnp.dot((b_float * begin_weight[:, None]).T, x_float, precision=lax.Precision.HIGHEST)
    return (y_local, state_end, state_begin)

def block_terms(inputs, step_bias, decay_log):
    x_block, bc_block, step_block, start_block = inputs
    row_count = x_block.shape[0]
    b_float = bc_block[:, :N].astype(jnp.float32)
    step_size = jax.nn.softplus(step_block.astype(jnp.float32) + step_bias[None, :])
    log_decay = -jnp.exp(decay_log)[None, :] * step_size
    cum_decay = jnp.cumsum(log_decay, axis=0)
    doc_index = jnp.cumsum(start_block, axis=0)
    scores = jnp.dot(bc_block[:, N:], bc_block[:, :N].T, preferred_element_type=jnp.float32)
    places = jnp.arange(row_count, dtype=jnp.int32)
    same_doc = ((doc_index[:, None] == doc_index[None, :]) & (places[:, None] != places[None, :])).astype(jnp.float32)
    heads_x = x_block.reshape(row_count, H, P_SIZE).transpose(1, 0, 2)
    y_local, state_end, state_begin = lax.map(lambda item: head_terms(item, scores, same_doc, doc_index, b_float), (cum_decay.T, step_size.T, heads_x))
    carry_gain = jnp.exp(cum_decay[-1]) * (doc_index[-1] == 0)
    left_gate = jnp.exp(cum_decay) * (doc_index == 0)[:, None]
    right_gate = jnp.exp(cum_decay[-1][None, :] - cum_decay) * (doc_index == doc_index[-1])[:, None]
    return (y_local.transpose(1, 0, 2), carry_gain, state_end, state_begin, left_gate, right_gate)

def reference(tokens_in, positions, doc_start, feature_weight, state_weight, step_weight, step_bias, decay_log, skip_gain, norm_gain):
    sequence_ids = jnp.arange(SEQS, dtype=jnp.int32)[:, None]
    ordered = jnp.zeros_like(tokens_in).at[sequence_ids, positions.astype(jnp.int32)].set(tokens_in)

    def one_sequence(inputs):
        features, starts = inputs
        x_proj = jnp.dot(features, feature_weight, preferred_element_type=jnp.float32).astype(jnp.bfloat16)
        bc_proj = jnp.dot(features, state_weight, preferred_element_type=jnp.float32).astype(jnp.bfloat16)
        step_raw = jnp.dot(features, step_weight, preferred_element_type=jnp.float32).astype(jnp.bfloat16)
        block_count = L // TOK_DEV
        blocks = (x_proj.reshape(block_count, TOK_DEV, H * P_SIZE), bc_proj.reshape(block_count, TOK_DEV, 2 * N), step_raw.reshape(block_count, TOK_DEV, H), starts.reshape(block_count, TOK_DEV))
        y_local, carry_gain, state_end, state_begin, left_gate, right_gate = lax.map(lambda item: block_terms(item, step_bias, decay_log), blocks)

        def advance(state, inputs):
            gain, ending = inputs
            return (gain[:, None, None] * state + ending, state)
        zero_state = jnp.zeros((H, N, P_SIZE), jnp.float32)
        _, state_in = lax.scan(advance, zero_state, (carry_gain, state_end))
        _, state_back = lax.scan(advance, zero_state, (carry_gain, state_begin), reverse=True)
        c_float = bc_proj[:, N:].astype(jnp.float32).reshape(block_count, TOK_DEV, N)
        from_left = jnp.einsum('btn,bhnp->bthp', c_float, state_in, precision=lax.Precision.HIGHEST)
        from_right = jnp.einsum('btn,bhnp->bthp', c_float, state_back, precision=lax.Precision.HIGHEST)
        x_heads = x_proj.reshape(block_count, TOK_DEV, H, P_SIZE).astype(jnp.float32)
        mixer = y_local + left_gate[..., None] * from_left + right_gate[..., None] * from_right + skip_gain[None, None, :, None] * x_heads
        mixer_rows = mixer.reshape(L, H * P_SIZE)
        mean_square = lax.optimization_barrier(jnp.sum(mixer_rows * mixer_rows, axis=1)) / (H * P_SIZE)
        return (mixer_rows * lax.rsqrt(mean_square + 1e-05)[:, None] * norm_gain[None, :]).astype(jnp.bfloat16)
    return lax.map(one_sequence, (ordered, doc_start))
```

```python
import jax
import jax.numpy as jnp
from jax import lax
from jax.sharding import PartitionSpec as P

HIGH = lax.Precision.HIGHEST


def carried(gains, states, here, reverse):
    count = gains.shape[0]
    k = jnp.arange(count)[:, None]
    u = jnp.arange(count)[None, :]
    if reverse:
        source = k > here
        between = (u > here) & (u < k)
    else:
        source = k < here
        between = (u > k) & (u < here)
    factors = jnp.where(between[:, :, None], gains[None, :, :], 1.0)
    weight = jnp.prod(factors, axis=1) * source.astype(jnp.float32)
    return jnp.sum(weight[:, :, None, None] * states, axis=0)


def per_device(
    tokens_in,
    positions,
    doc_start,
    feature_weight,
    state_weight,
    step_weight,
    step_bias,
    decay_log,
    skip_gain,
    norm_gain,
):
    row_count = tokens_in.shape[1]
    width = tokens_in.shape[2]
    shards = lax.axis_size("seq")
    here = lax.axis_index("seq")
    slot = row_count // shards
    rows = tokens_in[0].reshape(shards, slot, width)
    moved_rows = lax.all_to_all(rows, "seq", 0, 0, tiled=True).reshape(row_count, width)
    moved_positions = lax.all_to_all(
        positions[0].reshape(shards, slot), "seq", 0, 0, tiled=True
    ).reshape(row_count)
    offsets = moved_positions - here * row_count
    inverse = jnp.zeros((row_count,), jnp.int32).at[offsets].set(
        jnp.arange(row_count, dtype=jnp.int32)
    )
    features = moved_rows[inverse]

    head_count = step_bias.shape[0]
    feat_cols = feature_weight.shape[1]
    head_size = feat_cols // head_count
    state_size = state_weight.shape[1] // 2
    weights = jnp.concatenate([feature_weight, state_weight, step_weight], axis=1)
    gathered = lax.all_gather(weights, ("seq", "dp"), axis=0, tiled=True)
    proj = jnp.dot(features, gathered, preferred_element_type=jnp.float32).astype(jnp.bfloat16)
    x_proj = proj[:, :feat_cols]
    bc_proj = proj[:, feat_cols : feat_cols + 2 * state_size]
    step_raw = proj[:, feat_cols + 2 * state_size :]

    b_float = bc_proj[:, :state_size].astype(jnp.float32)
    c_float = bc_proj[:, state_size:].astype(jnp.float32)
    step_size = jax.nn.softplus(step_raw.astype(jnp.float32) + step_bias[None, :])
    log_decay = -jnp.exp(decay_log)[None, :] * step_size
    cum_decay = jnp.cumsum(log_decay, axis=0)
    doc_index = jnp.cumsum(doc_start[0], axis=0)
    scores = jnp.dot(
        bc_proj[:, state_size:], bc_proj[:, :state_size].T, preferred_element_type=jnp.float32
    )
    places = jnp.arange(row_count, dtype=jnp.int32)
    same_doc = (
        (doc_index[:, None] == doc_index[None, :]) & (places[:, None] != places[None, :])
    ).astype(jnp.float32)
    cum_t = cum_decay.T
    step_t = step_size.T
    decay = jnp.exp(-jnp.abs(cum_t[:, :, None] - cum_t[:, None, :])) * same_doc[None]
    mixing = scores[None] * decay * step_t[:, None, :]
    x_heads = x_proj.reshape(row_count, head_count, head_size).astype(jnp.float32)
    y_local = jnp.einsum("hts,shp->thp", mixing, x_heads, precision=HIGH)

    last_doc = (doc_index == doc_index[-1]).astype(jnp.float32)
    first_doc = (doc_index == 0).astype(jnp.float32)
    end_weight = jnp.exp(cum_decay[-1][None, :] - cum_decay) * last_doc[:, None] * step_size
    begin_weight = jnp.exp(cum_decay) * first_doc[:, None] * step_size
    state_end = jnp.einsum("tn,th,thp->hnp", b_float, end_weight, x_heads, precision=HIGH)
    state_begin = jnp.einsum("tn,th,thp->hnp", b_float, begin_weight, x_heads, precision=HIGH)
    carry_gain = jnp.exp(cum_decay[-1]) * (doc_index[-1] == 0)

    state_rows = 2 * head_count * state_size
    gain_rows = jnp.zeros((8, head_size), jnp.float32).at[0, :head_count].set(carry_gain)
    packed = jnp.concatenate(
        [state_end.reshape(-1, head_size), state_begin.reshape(-1, head_size), gain_rows]
    )
    every = lax.all_gather(packed, "seq", axis=0, tiled=True).reshape(shards, -1, head_size)
    gains = every[:, state_rows, :head_count]
    state_shape = (shards,) + state_end.shape
    ends = every[:, : state_rows // 2].reshape(state_shape)
    begins = every[:, state_rows // 2 : state_rows].reshape(state_shape)
    prefix = carried(gains, ends, here, False)
    suffix = carried(gains, begins, here, True)

    left_gate = jnp.exp(cum_decay) * first_doc[:, None]
    right_gate = jnp.exp(cum_decay[-1][None, :] - cum_decay) * last_doc[:, None]
    from_left = jnp.einsum("tn,hnp->thp", c_float, prefix, precision=HIGH)
    from_right = jnp.einsum("tn,hnp->thp", c_float, suffix, precision=HIGH)
    mixer = (
        y_local
        + left_gate[:, :, None] * from_left
        + right_gate[:, :, None] * from_right
        + skip_gain[None, :, None] * x_heads
    )
    mixer_rows = mixer.reshape(row_count, head_count * head_size)
    square_sum = lax.psum(jnp.sum(mixer_rows * mixer_rows, axis=1), "head")
    full_width = mixer_rows.shape[1] * lax.axis_size("head")
    inv_scale = lax.rsqrt(square_sum / full_width + 1e-05)
    return (mixer_rows * inv_scale[:, None] * norm_gain[None, :]).astype(jnp.bfloat16)[None]


def solution(mesh):
    placed = (
        P(("grp", "dp"), "seq", None),
        P(("grp", "dp"), "seq"),
        P(("grp", "dp"), "seq"),
        P(("seq", "dp"), "head"),
        P(("seq", "dp"), None),
        P(("seq", "dp"), "head"),
        P("head"),
        P("head"),
        P("head"),
        P("head"),
    )
    return jax.shard_map(
        per_device,
        mesh=mesh,
        in_specs=placed,
        out_specs=P(("grp", "dp"), "seq", "head"),
        check_vma=False,
    )
```

```python
import jax
import jax.numpy as jnp
from jax import lax
from jax.sharding import PartitionSpec as P

HIGH = lax.Precision.HIGHEST


def carried(gain, state, axis, reverse):
    count = lax.axis_size(axis)
    here = lax.axis_index(axis)
    rows = state.shape[0] * state.shape[1]
    pad = jnp.zeros((8, state.shape[2]), state.dtype).at[0, : gain.shape[0]].set(gain)
    value = jnp.concatenate([state.reshape(rows, -1), pad])

    def shift(x, step):
        if reverse:
            pairs = [(j, j - step) for j in range(step, count)]
            reached = here < count - step
        else:
            pairs = [(j, j + step) for j in range(count - step)]
            reached = here >= step
        return lax.ppermute(x, axis, pairs), reached

    value, reached = shift(value, 1)
    value = value.at[rows].set(jnp.where(reached, value[rows], 1.0))
    step = 1
    while step < count:
        earlier, reached = shift(value, step)
        g_early = jnp.where(reached, earlier[rows, : gain.shape[0]], 1.0)
        g_late = value[rows, : gain.shape[0]]
        late = value[:rows].reshape(state.shape)
        merged = g_late[:, None, None] * earlier[:rows].reshape(state.shape) + late
        value = jnp.concatenate(
            [merged.reshape(rows, -1), value[rows:].at[0, : gain.shape[0]].set(g_early * g_late)]
        )
        step *= 2
    return value[:rows].reshape(state.shape)


def per_device(
    tokens_in,
    positions,
    doc_start,
    feature_weight,
    state_weight,
    step_weight,
    step_bias,
    decay_log,
    skip_gain,
    norm_gain,
):
    row_count = tokens_in.shape[1]
    width = tokens_in.shape[2]
    shards = lax.axis_size("seq")
    here = lax.axis_index("seq")
    slot = row_count // shards
    rows = tokens_in[0].reshape(shards, slot, width)
    moved_rows = lax.all_to_all(rows, "seq", 0, 0, tiled=True).reshape(row_count, width)
    moved_positions = lax.all_to_all(
        positions[0].reshape(shards, slot), "seq", 0, 0, tiled=True
    ).reshape(row_count)
    offsets = moved_positions - here * row_count
    inverse = jnp.zeros((row_count,), jnp.int32).at[offsets].set(
        jnp.arange(row_count, dtype=jnp.int32)
    )
    features = moved_rows[inverse]

    head_count = step_bias.shape[0]
    feat_cols = feature_weight.shape[1]
    head_size = feat_cols // head_count
    state_size = state_weight.shape[1] // 2
    weights = jnp.concatenate([feature_weight, state_weight, step_weight], axis=1)
    gathered = lax.all_gather(weights, ("seq", "dp"), axis=0, tiled=True)
    proj = jnp.dot(features, gathered, preferred_element_type=jnp.float32).astype(jnp.bfloat16)
    x_proj = proj[:, :feat_cols]
    bc_proj = proj[:, feat_cols : feat_cols + 2 * state_size]
    step_raw = proj[:, feat_cols + 2 * state_size :]

    b_float = bc_proj[:, :state_size].astype(jnp.float32)
    c_float = bc_proj[:, state_size:].astype(jnp.float32)
    step_size = jax.nn.softplus(step_raw.astype(jnp.float32) + step_bias[None, :])
    log_decay = -jnp.exp(decay_log)[None, :] * step_size
    cum_decay = jnp.cumsum(log_decay, axis=0)
    doc_index = jnp.cumsum(doc_start[0], axis=0)
    scores = jnp.dot(
        bc_proj[:, state_size:], bc_proj[:, :state_size].T, preferred_element_type=jnp.float32
    )
    places = jnp.arange(row_count, dtype=jnp.int32)
    same_doc = (
        (doc_index[:, None] == doc_index[None, :]) & (places[:, None] != places[None, :])
    ).astype(jnp.float32)
    cum_t = cum_decay.T
    step_t = step_size.T
    decay = jnp.exp(-jnp.abs(cum_t[:, :, None] - cum_t[:, None, :])) * same_doc[None]
    mixing = scores[None] * decay * step_t[:, None, :]
    x_heads = x_proj.reshape(row_count, head_count, head_size).astype(jnp.float32)
    y_local = jnp.einsum("hts,shp->thp", mixing, x_heads, precision=HIGH)

    last_doc = (doc_index == doc_index[-1]).astype(jnp.float32)
    first_doc = (doc_index == 0).astype(jnp.float32)
    end_weight = jnp.exp(cum_decay[-1][None, :] - cum_decay) * last_doc[:, None] * step_size
    begin_weight = jnp.exp(cum_decay) * first_doc[:, None] * step_size
    state_end = jnp.einsum("tn,th,thp->hnp", b_float, end_weight, x_heads, precision=HIGH)
    state_begin = jnp.einsum("tn,th,thp->hnp", b_float, begin_weight, x_heads, precision=HIGH)
    carry_gain = jnp.exp(cum_decay[-1]) * (doc_index[-1] == 0)

    prefix = carried(carry_gain, state_end, "seq", False)
    suffix = carried(carry_gain, state_begin, "seq", True)

    left_gate = jnp.exp(cum_decay) * first_doc[:, None]
    right_gate = jnp.exp(cum_decay[-1][None, :] - cum_decay) * last_doc[:, None]
    from_left = jnp.einsum("tn,hnp->thp", c_float, prefix, precision=HIGH)
    from_right = jnp.einsum("tn,hnp->thp", c_float, suffix, precision=HIGH)
    mixer = (
        y_local
        + left_gate[:, :, None] * from_left
        + right_gate[:, :, None] * from_right
        + skip_gain[None, :, None] * x_heads
    )
    mixer_rows = mixer.reshape(row_count, head_count * head_size)
    square_sum = lax.psum(jnp.sum(mixer_rows * mixer_rows, axis=1), "head")
    full_width = mixer_rows.shape[1] * lax.axis_size("head")
    inv_scale = lax.rsqrt(square_sum / full_width + 1e-05)
    return (mixer_rows * inv_scale[:, None] * norm_gain[None, :]).astype(jnp.bfloat16)[None]


def solution(mesh):
    placed = (
        P(("grp", "dp"), "seq", None),
        P(("grp", "dp"), "seq"),
        P(("grp", "dp"), "seq"),
        P(("seq", "dp"), "head"),
        P(("seq", "dp"), None),
        P(("seq", "dp"), "head"),
        P("head"),
        P("head"),
        P("head"),
        P("head"),
    )
    return jax.shard_map(
        per_device,
        mesh=mesh,
        in_specs=placed,
        out_specs=P(("grp", "dp"), "seq", "head"),
        check_vma=False,
    )
```

```python
import jax
import jax.numpy as jnp
from jax import lax
from jax.sharding import PartitionSpec as P

HIGH = lax.Precision.HIGHEST


def carried(gain, state, axis, reverse):
    count = lax.axis_size(axis)
    here = lax.axis_index(axis)
    rows = state.shape[0] * state.shape[1]
    pad = jnp.zeros((8, state.shape[2]), state.dtype).at[0, : gain.shape[0]].set(gain)
    value = jnp.concatenate([state.reshape(rows, -1), pad])

    def shift(x, step):
        if reverse:
            pairs = [(j, j - step) for j in range(step, count)]
            reached = here < count - step
        else:
            pairs = [(j, j + step) for j in range(count - step)]
            reached = here >= step
        return lax.ppermute(x, axis, pairs), reached

    value, reached = shift(value, 1)
    value = value.at[rows].set(jnp.where(reached, value[rows], 1.0))
    step = 1
    while step < count:
        earlier, reached = shift(value, step)
        g_early = jnp.where(reached, earlier[rows, : gain.shape[0]], 1.0)
        g_late = value[rows, : gain.shape[0]]
        late = value[:rows].reshape(state.shape)
        merged = g_late[:, None, None] * earlier[:rows].reshape(state.shape) + late
        value = jnp.concatenate(
            [merged.reshape(rows, -1), value[rows:].at[0, : gain.shape[0]].set(g_early * g_late)]
        )
        step *= 2
    return value[:rows].reshape(state.shape)


def per_device(
    tokens_in,
    positions,
    doc_start,
    feature_weight,
    state_weight,
    step_weight,
    step_bias,
    decay_log,
    skip_gain,
    norm_gain,
):
    row_count = tokens_in.shape[1]
    width = tokens_in.shape[2]
    shards = lax.axis_size("seq")
    here = lax.axis_index("seq")
    slot = row_count // shards
    rows = tokens_in[0].reshape(shards, slot, width)
    moved_rows = lax.all_to_all(rows, "seq", 0, 0, tiled=True).reshape(row_count, width)
    moved_positions = lax.all_to_all(
        positions[0].reshape(shards, slot), "seq", 0, 0, tiled=True
    ).reshape(row_count)
    offsets = moved_positions - here * row_count
    inverse = jnp.zeros((row_count,), jnp.int32).at[offsets].set(
        jnp.arange(row_count, dtype=jnp.int32)
    )
    features = moved_rows[inverse]

    head_count = step_bias.shape[0]
    feat_cols = feature_weight.shape[1]
    head_size = feat_cols // head_count
    state_size = state_weight.shape[1] // 2
    seq_count = lax.axis_size("seq")
    dp_count = lax.axis_size("dp")
    block_rows = feature_weight.shape[0]
    weights = jnp.concatenate([feature_weight, state_weight, step_weight], axis=1)
    gathered = lax.all_gather(weights, "seq", axis=0, tiled=True)
    parts = features.reshape(row_count, seq_count, dp_count, block_rows).transpose(2, 0, 1, 3)
    mine = lax.all_to_all(parts, "dp", 0, 0, tiled=True)
    mine = mine.reshape(dp_count * row_count, seq_count * block_rows)
    partial = jnp.dot(mine, gathered, preferred_element_type=jnp.float32)
    proj = lax.psum_scatter(partial, "dp", scatter_dimension=0, tiled=True).astype(jnp.bfloat16)
    x_proj = proj[:, :feat_cols]
    bc_proj = proj[:, feat_cols : feat_cols + 2 * state_size]
    step_raw = proj[:, feat_cols + 2 * state_size :]

    b_float = bc_proj[:, :state_size].astype(jnp.float32)
    c_float = bc_proj[:, state_size:].astype(jnp.float32)
    step_size = jax.nn.softplus(step_raw.astype(jnp.float32) + step_bias[None, :])
    log_decay = -jnp.exp(decay_log)[None, :] * step_size
    cum_decay = jnp.cumsum(log_decay, axis=0)
    doc_index = jnp.cumsum(doc_start[0], axis=0)
    scores = jnp.dot(
        bc_proj[:, state_size:], bc_proj[:, :state_size].T, preferred_element_type=jnp.float32
    )
    places = jnp.arange(row_count, dtype=jnp.int32)
    same_doc = (
        (doc_index[:, None] == doc_index[None, :]) & (places[:, None] != places[None, :])
    ).astype(jnp.float32)
    cum_t = cum_decay.T
    step_t = step_size.T
    decay = jnp.exp(-jnp.abs(cum_t[:, :, None] - cum_t[:, None, :])) * same_doc[None]
    mixing = scores[None] * decay * step_t[:, None, :]
    x_heads = x_proj.reshape(row_count, head_count, head_size).astype(jnp.float32)
    y_local = jnp.einsum("hts,shp->thp", mixing, x_heads, precision=HIGH)

    last_doc = (doc_index == doc_index[-1]).astype(jnp.float32)
    first_doc = (doc_index == 0).astype(jnp.float32)
    end_weight = jnp.exp(cum_decay[-1][None, :] - cum_decay) * last_doc[:, None] * step_size
    begin_weight = jnp.exp(cum_decay) * first_doc[:, None] * step_size
    state_end = jnp.einsum("tn,th,thp->hnp", b_float, end_weight, x_heads, precision=HIGH)
    state_begin = jnp.einsum("tn,th,thp->hnp", b_float, begin_weight, x_heads, precision=HIGH)
    carry_gain = jnp.exp(cum_decay[-1]) * (doc_index[-1] == 0)

    prefix = carried(carry_gain, state_end, "seq", False)
    suffix = carried(carry_gain, state_begin, "seq", True)

    left_gate = jnp.exp(cum_decay) * first_doc[:, None]
    right_gate = jnp.exp(cum_decay[-1][None, :] - cum_decay) * last_doc[:, None]
    from_left = jnp.einsum("tn,hnp->thp", c_float, prefix, precision=HIGH)
    from_right = jnp.einsum("tn,hnp->thp", c_float, suffix, precision=HIGH)
    mixer = (
        y_local
        + left_gate[:, :, None] * from_left
        + right_gate[:, :, None] * from_right
        + skip_gain[None, :, None] * x_heads
    )
    mixer_rows = mixer.reshape(row_count, head_count * head_size)
    square_sum = lax.psum(jnp.sum(mixer_rows * mixer_rows, axis=1), "head")
    full_width = mixer_rows.shape[1] * lax.axis_size("head")
    inv_scale = lax.rsqrt(square_sum / full_width + 1e-05)
    return (mixer_rows * inv_scale[:, None] * norm_gain[None, :]).astype(jnp.bfloat16)[None]


def solution(mesh):
    placed = (
        P(("grp", "dp"), "seq", None),
        P(("grp", "dp"), "seq"),
        P(("grp", "dp"), "seq"),
        P(("seq", "dp"), "head"),
        P(("seq", "dp"), None),
        P(("seq", "dp"), "head"),
        P("head"),
        P("head"),
        P("head"),
        P("head"),
    )
    return jax.shard_map(
        per_device,
        mesh=mesh,
        in_specs=placed,
        out_specs=P(("grp", "dp"), "seq", "head"),
        check_vma=False,
    )
```

```python
import jax
import jax.numpy as jnp
from jax import lax
from jax.sharding import PartitionSpec as P

HIGH = lax.Precision.HIGHEST


def carried(gain, state, axis, reverse):
    count = lax.axis_size(axis)
    here = lax.axis_index(axis)
    rows = state.shape[0] * state.shape[1]
    pad = jnp.zeros((8, state.shape[2]), state.dtype).at[0, : gain.shape[0]].set(gain)
    value = jnp.concatenate([state.reshape(rows, -1), pad])

    def shift(x, step):
        if reverse:
            pairs = [(j, j - step) for j in range(step, count)]
            reached = here < count - step
        else:
            pairs = [(j, j + step) for j in range(count - step)]
            reached = here >= step
        return lax.ppermute(x, axis, pairs), reached

    value, reached = shift(value, 1)
    value = value.at[rows].set(jnp.where(reached, value[rows], 1.0))
    step = 1
    while step < count:
        earlier, reached = shift(value, step)
        g_early = jnp.where(reached, earlier[rows, : gain.shape[0]], 1.0)
        g_late = value[rows, : gain.shape[0]]
        late = value[:rows].reshape(state.shape)
        merged = g_late[:, None, None] * earlier[:rows].reshape(state.shape) + late
        value = jnp.concatenate(
            [merged.reshape(rows, -1), value[rows:].at[0, : gain.shape[0]].set(g_early * g_late)]
        )
        step *= 2
    return value[:rows].reshape(state.shape)


def per_device(
    tokens_in,
    positions,
    doc_start,
    feature_weight,
    state_weight,
    step_weight,
    step_bias,
    decay_log,
    skip_gain,
    norm_gain,
):
    row_count = tokens_in.shape[1]
    shards = lax.axis_size("seq")
    here = lax.axis_index("seq")
    slot = row_count // shards
    head_count = step_bias.shape[0]
    feat_cols = feature_weight.shape[1]
    head_size = feat_cols // head_count
    state_size = state_weight.shape[1] // 2

    seq_count = lax.axis_size("seq")
    dp_count = lax.axis_size("dp")
    block_rows = feature_weight.shape[0]
    weights = jnp.concatenate([feature_weight, state_weight, step_weight], axis=1)
    gathered = lax.all_gather(weights, "seq", axis=0, tiled=True)
    parts = tokens_in[0].reshape(row_count, seq_count, dp_count, block_rows).transpose(2, 0, 1, 3)
    mine = lax.all_to_all(parts, "dp", 0, 0, tiled=True)
    mine = mine.reshape(dp_count * row_count, seq_count * block_rows)
    partial = jnp.dot(mine, gathered, preferred_element_type=jnp.float32)
    projected = lax.psum_scatter(partial, "dp", scatter_dimension=0, tiled=True)
    projected = projected.astype(jnp.bfloat16).reshape(shards, slot, -1)
    moved = lax.all_to_all(projected, "seq", 0, 0, tiled=True).reshape(row_count, -1)
    moved_positions = lax.all_to_all(
        positions[0].reshape(shards, slot), "seq", 0, 0, tiled=True
    ).reshape(row_count)
    offsets = moved_positions - here * row_count
    inverse = jnp.zeros((row_count,), jnp.int32).at[offsets].set(
        jnp.arange(row_count, dtype=jnp.int32)
    )
    proj = moved[inverse]
    x_proj = proj[:, :feat_cols]
    bc_proj = proj[:, feat_cols : feat_cols + 2 * state_size]
    step_raw = proj[:, feat_cols + 2 * state_size :]

    b_float = bc_proj[:, :state_size].astype(jnp.float32)
    c_float = bc_proj[:, state_size:].astype(jnp.float32)
    step_size = jax.nn.softplus(step_raw.astype(jnp.float32) + step_bias[None, :])
    log_decay = -jnp.exp(decay_log)[None, :] * step_size
    cum_decay = jnp.cumsum(log_decay, axis=0)
    doc_index = jnp.cumsum(doc_start[0], axis=0)
    scores = jnp.dot(
        bc_proj[:, state_size:], bc_proj[:, :state_size].T, preferred_element_type=jnp.float32
    )
    places = jnp.arange(row_count, dtype=jnp.int32)
    same_doc = (
        (doc_index[:, None] == doc_index[None, :]) & (places[:, None] != places[None, :])
    ).astype(jnp.float32)
    cum_t = cum_decay.T
    step_t = step_size.T
    decay = jnp.exp(-jnp.abs(cum_t[:, :, None] - cum_t[:, None, :])) * same_doc[None]
    mixing = scores[None] * decay * step_t[:, None, :]
    x_heads = x_proj.reshape(row_count, head_count, head_size).astype(jnp.float32)
    y_local = jnp.einsum("hts,shp->thp", mixing, x_heads, precision=HIGH)

    last_doc = (doc_index == doc_index[-1]).astype(jnp.float32)
    first_doc = (doc_index == 0).astype(jnp.float32)
    end_weight = jnp.exp(cum_decay[-1][None, :] - cum_decay) * last_doc[:, None] * step_size
    begin_weight = jnp.exp(cum_decay) * first_doc[:, None] * step_size
    state_end = jnp.einsum("tn,th,thp->hnp", b_float, end_weight, x_heads, precision=HIGH)
    state_begin = jnp.einsum("tn,th,thp->hnp", b_float, begin_weight, x_heads, precision=HIGH)
    carry_gain = jnp.exp(cum_decay[-1]) * (doc_index[-1] == 0)

    prefix = carried(carry_gain, state_end, "seq", False)
    suffix = carried(carry_gain, state_begin, "seq", True)

    left_gate = jnp.exp(cum_decay) * first_doc[:, None]
    right_gate = jnp.exp(cum_decay[-1][None, :] - cum_decay) * last_doc[:, None]
    from_left = jnp.einsum("tn,hnp->thp", c_float, prefix, precision=HIGH)
    from_right = jnp.einsum("tn,hnp->thp", c_float, suffix, precision=HIGH)
    mixer = (
        y_local
        + left_gate[:, :, None] * from_left
        + right_gate[:, :, None] * from_right
        + skip_gain[None, :, None] * x_heads
    )
    mixer_rows = mixer.reshape(row_count, head_count * head_size)
    square_sum = lax.psum(jnp.sum(mixer_rows * mixer_rows, axis=1), "head")
    full_width = mixer_rows.shape[1] * lax.axis_size("head")
    inv_scale = lax.rsqrt(square_sum / full_width + 1e-05)
    return (mixer_rows * inv_scale[:, None] * norm_gain[None, :]).astype(jnp.bfloat16)[None]


def solution(mesh):
    placed = (
        P(("grp", "dp"), "seq", None),
        P(("grp", "dp"), "seq"),
        P(("grp", "dp"), "seq"),
        P(("seq", "dp"), "head"),
        P(("seq", "dp"), None),
        P(("seq", "dp"), "head"),
        P("head"),
        P("head"),
        P("head"),
        P("head"),
    )
    return jax.shard_map(
        per_device,
        mesh=mesh,
        in_specs=placed,
        out_specs=P(("grp", "dp"), "seq", "head"),
        check_vma=False,
    )
```

```python
import jax
import jax.numpy as jnp
from jax import lax
from jax.sharding import PartitionSpec as P

HIGH = lax.Precision.HIGHEST


def carried(gain, state, axis, reverse):
    count = lax.axis_size(axis)
    rows = state.shape[0] * state.shape[1]
    heads = gain.shape[0]
    pad = jnp.zeros((8, state.shape[2]), state.dtype).at[0, :heads].set(gain)
    value = jnp.concatenate([state.reshape(rows, -1), pad])
    total = jnp.zeros(state.shape, state.dtype)
    factor = jnp.ones((heads,), state.dtype)
    for step in range(1, count):
        if reverse:
            pairs = [(j, j - step) for j in range(step, count)]
        else:
            pairs = [(j, j + step) for j in range(count - step)]
        got = lax.ppermute(value, axis, pairs)
        total = total + factor[:, None, None] * got[:rows].reshape(state.shape)
        factor = factor * got[rows, :heads]
    return total


def per_device(
    tokens_in,
    positions,
    doc_start,
    feature_weight,
    state_weight,
    step_weight,
    step_bias,
    decay_log,
    skip_gain,
    norm_gain,
):
    row_count = tokens_in.shape[1]
    shards = lax.axis_size("seq")
    here = lax.axis_index("seq")
    slot = row_count // shards
    head_count = step_bias.shape[0]
    feat_cols = feature_weight.shape[1]
    head_size = feat_cols // head_count
    state_size = state_weight.shape[1] // 2

    seq_count = lax.axis_size("seq")
    dp_count = lax.axis_size("dp")
    block_rows = feature_weight.shape[0]
    weights = jnp.concatenate([feature_weight, state_weight, step_weight], axis=1)
    gathered = lax.all_gather(weights, "seq", axis=0, tiled=True)
    parts = tokens_in[0].reshape(row_count, seq_count, dp_count, block_rows).transpose(2, 0, 1, 3)
    mine = lax.all_to_all(parts, "dp", 0, 0, tiled=True)
    mine = mine.reshape(dp_count * row_count, seq_count * block_rows)
    partial = jnp.dot(mine, gathered, preferred_element_type=jnp.float32)
    projected = lax.psum_scatter(partial, "dp", scatter_dimension=0, tiled=True)
    projected = projected.astype(jnp.bfloat16).reshape(shards, slot, -1)
    moved = lax.all_to_all(projected, "seq", 0, 0, tiled=True).reshape(row_count, -1)
    moved_positions = lax.all_to_all(
        positions[0].reshape(shards, slot), "seq", 0, 0, tiled=True
    ).reshape(row_count)
    offsets = moved_positions - here * row_count
    inverse = jnp.zeros((row_count,), jnp.int32).at[offsets].set(
        jnp.arange(row_count, dtype=jnp.int32)
    )
    proj = moved[inverse]
    x_proj = proj[:, :feat_cols]
    bc_proj = proj[:, feat_cols : feat_cols + 2 * state_size]
    step_raw = proj[:, feat_cols + 2 * state_size :]

    b_float = bc_proj[:, :state_size].astype(jnp.float32)
    c_float = bc_proj[:, state_size:].astype(jnp.float32)
    step_size = jax.nn.softplus(step_raw.astype(jnp.float32) + step_bias[None, :])
    log_decay = -jnp.exp(decay_log)[None, :] * step_size
    cum_decay = jnp.cumsum(log_decay, axis=0)
    doc_index = jnp.cumsum(doc_start[0], axis=0)
    scores = jnp.dot(
        bc_proj[:, state_size:], bc_proj[:, :state_size].T, preferred_element_type=jnp.float32
    )
    places = jnp.arange(row_count, dtype=jnp.int32)
    same_doc = (
        (doc_index[:, None] == doc_index[None, :]) & (places[:, None] != places[None, :])
    ).astype(jnp.float32)
    cum_t = cum_decay.T
    step_t = step_size.T
    decay = jnp.exp(-jnp.abs(cum_t[:, :, None] - cum_t[:, None, :])) * same_doc[None]
    mixing = scores[None] * decay * step_t[:, None, :]
    x_heads = x_proj.reshape(row_count, head_count, head_size).astype(jnp.float32)
    y_local = jnp.einsum("hts,shp->thp", mixing, x_heads, precision=HIGH)

    last_doc = (doc_index == doc_index[-1]).astype(jnp.float32)
    first_doc = (doc_index == 0).astype(jnp.float32)
    end_weight = jnp.exp(cum_decay[-1][None, :] - cum_decay) * last_doc[:, None] * step_size
    begin_weight = jnp.exp(cum_decay) * first_doc[:, None] * step_size
    state_end = jnp.einsum("tn,th,thp->hnp", b_float, end_weight, x_heads, precision=HIGH)
    state_begin = jnp.einsum("tn,th,thp->hnp", b_float, begin_weight, x_heads, precision=HIGH)
    carry_gain = jnp.exp(cum_decay[-1]) * (doc_index[-1] == 0)

    prefix = carried(carry_gain, state_end, "seq", False)
    suffix = carried(carry_gain, state_begin, "seq", True)

    left_gate = jnp.exp(cum_decay) * first_doc[:, None]
    right_gate = jnp.exp(cum_decay[-1][None, :] - cum_decay) * last_doc[:, None]
    from_left = jnp.einsum("tn,hnp->thp", c_float, prefix, precision=HIGH)
    from_right = jnp.einsum("tn,hnp->thp", c_float, suffix, precision=HIGH)
    mixer = (
        y_local
        + left_gate[:, :, None] * from_left
        + right_gate[:, :, None] * from_right
        + skip_gain[None, :, None] * x_heads
    )
    mixer_rows = mixer.reshape(row_count, head_count * head_size)
    square_sum = lax.psum(jnp.sum(mixer_rows * mixer_rows, axis=1), "head")
    full_width = mixer_rows.shape[1] * lax.axis_size("head")
    inv_scale = lax.rsqrt(square_sum / full_width + 1e-05)
    return (mixer_rows * inv_scale[:, None] * norm_gain[None, :]).astype(jnp.bfloat16)[None]


def solution(mesh):
    placed = (
        P(("grp", "dp"), "seq", None),
        P(("grp", "dp"), "seq"),
        P(("grp", "dp"), "seq"),
        P(("seq", "dp"), "head"),
        P(("seq", "dp"), None),
        P(("seq", "dp"), "head"),
        P("head"),
        P("head"),
        P("head"),
        P("head"),
    )
    return jax.shard_map(
        per_device,
        mesh=mesh,
        in_specs=placed,
        out_specs=P(("grp", "dp"), "seq", "head"),
        check_vma=False,
    )
```

```python
import jax
import jax.numpy as jnp
from jax import lax
from jax.sharding import PartitionSpec as P

HIGH = lax.Precision.HIGHEST


def carried(gain, state, axis, reverse):
    count = lax.axis_size(axis)
    rows = state.shape[0] * state.shape[1]
    heads = gain.shape[0]
    pad = jnp.zeros((8, state.shape[2]), state.dtype).at[0, :heads].set(gain)
    value = jnp.concatenate([state.reshape(rows, -1), pad])
    total = jnp.zeros(state.shape, state.dtype)
    factor = jnp.ones((heads,), state.dtype)
    for step in range(1, count):
        if reverse:
            pairs = [(j, j - step) for j in range(step, count)]
        else:
            pairs = [(j, j + step) for j in range(count - step)]
        got = lax.ppermute(value, axis, pairs)
        total = total + factor[:, None, None] * got[:rows].reshape(state.shape)
        factor = factor * got[rows, :heads]
    return total


def per_device(
    tokens_in,
    positions,
    doc_start,
    feature_weight,
    state_weight,
    step_weight,
    step_bias,
    decay_log,
    skip_gain,
    norm_gain,
):
    row_count = tokens_in.shape[1]
    shards = lax.axis_size("seq")
    here = lax.axis_index("seq")
    slot = row_count // shards
    head_count = step_bias.shape[0]
    feat_cols = feature_weight.shape[1]
    head_size = feat_cols // head_count
    state_size = state_weight.shape[1] // 2

    seq_count = lax.axis_size("seq")
    dp_count = lax.axis_size("dp")
    block_rows = feature_weight.shape[0]
    parts = tokens_in[0].reshape(row_count, seq_count, dp_count, block_rows).transpose(2, 0, 1, 3)
    mine = lax.all_to_all(parts, "dp", 0, 0, tiled=True)
    mine = mine.reshape(dp_count * row_count, seq_count * block_rows)
    moved_positions = lax.all_to_all(
        positions[0].reshape(shards, slot), "seq", 0, 0, tiled=True
    ).reshape(row_count)
    offsets = moved_positions - here * row_count
    inverse = jnp.zeros((row_count,), jnp.int32).at[offsets].set(
        jnp.arange(row_count, dtype=jnp.int32)
    )

    def project(weights):
        spread = jnp.broadcast_to(weights[None], (seq_count,) + weights.shape)
        gathered = lax.all_to_all(spread, "seq", 0, 0, tiled=True)
        gathered = gathered.reshape(seq_count * block_rows, -1)
        partial = jnp.dot(mine, gathered, preferred_element_type=jnp.float32)
        projected = lax.psum_scatter(partial, "dp", scatter_dimension=0, tiled=True)
        projected = projected.astype(jnp.bfloat16).reshape(shards, slot, -1)
        moved = lax.all_to_all(projected, "seq", 0, 0, tiled=True).reshape(row_count, -1)
        return moved[inverse]

    split_heads = head_count // 2
    split = split_heads * head_size
    first = project(
        jnp.concatenate([state_weight, step_weight, feature_weight[:, :split]], axis=1)
    )
    second = project(feature_weight[:, split:])
    bc_proj = first[:, : 2 * state_size]
    step_raw = first[:, 2 * state_size : 2 * state_size + head_count]
    x_parts = (first[:, 2 * state_size + head_count :], second)

    b_float = bc_proj[:, :state_size].astype(jnp.float32)
    c_float = bc_proj[:, state_size:].astype(jnp.float32)
    step_size = jax.nn.softplus(step_raw.astype(jnp.float32) + step_bias[None, :])
    log_decay = -jnp.exp(decay_log)[None, :] * step_size
    cum_decay = jnp.cumsum(log_decay, axis=0)
    doc_index = jnp.cumsum(doc_start[0], axis=0)
    scores = jnp.dot(
        bc_proj[:, state_size:], bc_proj[:, :state_size].T, preferred_element_type=jnp.float32
    )
    places = jnp.arange(row_count, dtype=jnp.int32)
    same_doc = (
        (doc_index[:, None] == doc_index[None, :]) & (places[:, None] != places[None, :])
    ).astype(jnp.float32)
    last_doc = (doc_index == doc_index[-1]).astype(jnp.float32)
    first_doc = (doc_index == 0).astype(jnp.float32)

    def mix(x_part, lo, hi):
        cum = cum_decay[:, lo:hi]
        step = step_size[:, lo:hi]
        cum_t = cum.T
        decay = jnp.exp(-jnp.abs(cum_t[:, :, None] - cum_t[:, None, :])) * same_doc[None]
        mixing = scores[None] * decay * step.T[:, None, :]
        x_heads = x_part.reshape(row_count, hi - lo, head_size).astype(jnp.float32)
        y_local = jnp.einsum("hts,shp->thp", mixing, x_heads, precision=HIGH)
        end_weight = jnp.exp(cum[-1][None, :] - cum) * last_doc[:, None] * step
        begin_weight = jnp.exp(cum) * first_doc[:, None] * step
        state_end = jnp.einsum("tn,th,thp->hnp", b_float, end_weight, x_heads, precision=HIGH)
        state_begin = jnp.einsum("tn,th,thp->hnp", b_float, begin_weight, x_heads, precision=HIGH)
        carry_gain = jnp.exp(cum[-1]) * (doc_index[-1] == 0)
        prefix = carried(carry_gain, state_end, "seq", False)
        suffix = carried(carry_gain, state_begin, "seq", True)
        left_gate = jnp.exp(cum) * first_doc[:, None]
        right_gate = jnp.exp(cum[-1][None, :] - cum) * last_doc[:, None]
        from_left = jnp.einsum("tn,hnp->thp", c_float, prefix, precision=HIGH)
        from_right = jnp.einsum("tn,hnp->thp", c_float, suffix, precision=HIGH)
        return (
            y_local
            + left_gate[:, :, None] * from_left
            + right_gate[:, :, None] * from_right
            + skip_gain[None, lo:hi, None] * x_heads
        )

    mixer = jnp.concatenate(
        [mix(x_parts[0], 0, split_heads), mix(x_parts[1], split_heads, head_count)], axis=1
    )
    mixer_rows = mixer.reshape(row_count, head_count * head_size)
    square_sum = lax.psum(jnp.sum(mixer_rows * mixer_rows, axis=1), "head")
    full_width = mixer_rows.shape[1] * lax.axis_size("head")
    inv_scale = lax.rsqrt(square_sum / full_width + 1e-05)
    return (mixer_rows * inv_scale[:, None] * norm_gain[None, :]).astype(jnp.bfloat16)[None]


def solution(mesh):
    placed = (
        P(("grp", "dp"), "seq", None),
        P(("grp", "dp"), "seq"),
        P(("grp", "dp"), "seq"),
        P(("seq", "dp"), "head"),
        P(("seq", "dp"), None),
        P(("seq", "dp"), "head"),
        P("head"),
        P("head"),
        P("head"),
        P("head"),
    )
    return jax.shard_map(
        per_device,
        mesh=mesh,
        in_specs=placed,
        out_specs=P(("grp", "dp"), "seq", "head"),
        check_vma=False,
    )
```

```python
import jax
import jax.numpy as jnp
from jax import lax
from jax.sharding import PartitionSpec as P

HIGH = lax.Precision.HIGHEST


def carried(gain, state, axis, reverse):
    count = lax.axis_size(axis)
    rows = state.shape[0] * state.shape[1]
    heads = gain.shape[0]
    pad = jnp.zeros((8, state.shape[2]), state.dtype).at[0, :heads].set(gain)
    value = jnp.concatenate([state.reshape(rows, -1), pad])
    total = jnp.zeros(state.shape, state.dtype)
    factor = jnp.ones((heads,), state.dtype)
    for step in range(1, count):
        if reverse:
            pairs = [(j, j - step) for j in range(step, count)]
        else:
            pairs = [(j, j + step) for j in range(count - step)]
        got = lax.ppermute(value, axis, pairs)
        total = total + factor[:, None, None] * got[:rows].reshape(state.shape)
        factor = factor * got[rows, :heads]
    return total


def per_device(
    tokens_in,
    positions,
    doc_start,
    feature_weight,
    state_weight,
    step_weight,
    step_bias,
    decay_log,
    skip_gain,
    norm_gain,
):
    row_count = tokens_in.shape[1]
    shards = lax.axis_size("seq")
    here = lax.axis_index("seq")
    slot = row_count // shards
    head_count = step_bias.shape[0]
    feat_cols = feature_weight.shape[1]
    head_size = feat_cols // head_count
    state_size = state_weight.shape[1] // 2

    seq_count = lax.axis_size("seq")
    dp_count = lax.axis_size("dp")
    block_rows = feature_weight.shape[0]
    parts = tokens_in[0].reshape(row_count, seq_count, dp_count, block_rows).transpose(2, 0, 1, 3)
    mine = lax.all_to_all(parts, "dp", 0, 0, tiled=True)
    mine = mine.reshape(dp_count * row_count, seq_count * block_rows)
    moved_positions = lax.all_to_all(
        positions[0].reshape(shards, slot), "seq", 0, 0, tiled=True
    ).reshape(row_count)
    offsets = moved_positions - here * row_count
    inverse = jnp.zeros((row_count,), jnp.int32).at[offsets].set(
        jnp.arange(row_count, dtype=jnp.int32)
    )

    def gather_rows(weights, offloaded):
        if offloaded:
            return lax.all_gather(weights, "seq", axis=0, tiled=True)
        spread = jnp.broadcast_to(weights[None], (seq_count,) + weights.shape)
        gathered = lax.all_to_all(spread, "seq", 0, 0, tiled=True)
        return gathered.reshape(seq_count * block_rows, -1)

    def project(gathered):
        partial = jnp.dot(mine, gathered, preferred_element_type=jnp.float32)
        projected = lax.psum_scatter(partial, "dp", scatter_dimension=0, tiled=True)
        projected = projected.astype(jnp.bfloat16).reshape(shards, slot, -1)
        moved = lax.all_to_all(projected, "seq", 0, 0, tiled=True).reshape(row_count, -1)
        return moved[inverse]

    split_heads = head_count // 2
    split = split_heads * head_size
    gathered_first = gather_rows(
        jnp.concatenate([state_weight, step_weight, feature_weight[:, :split]], axis=1), True
    )
    rest, gathered_first = lax.optimization_barrier((feature_weight[:, split:], gathered_first))
    first = project(gathered_first)
    second = project(gather_rows(rest, False))
    bc_proj = first[:, : 2 * state_size]
    step_raw = first[:, 2 * state_size : 2 * state_size + head_count]
    x_parts = (first[:, 2 * state_size + head_count :], second)

    b_float = bc_proj[:, :state_size].astype(jnp.float32)
    c_float = bc_proj[:, state_size:].astype(jnp.float32)
    step_size = jax.nn.softplus(step_raw.astype(jnp.float32) + step_bias[None, :])
    log_decay = -jnp.exp(decay_log)[None, :] * step_size
    cum_decay = jnp.cumsum(log_decay, axis=0)
    doc_index = jnp.cumsum(doc_start[0], axis=0)
    scores = jnp.dot(
        bc_proj[:, state_size:], bc_proj[:, :state_size].T, preferred_element_type=jnp.float32
    )
    places = jnp.arange(row_count, dtype=jnp.int32)
    same_doc = (
        (doc_index[:, None] == doc_index[None, :]) & (places[:, None] != places[None, :])
    ).astype(jnp.float32)
    last_doc = (doc_index == doc_index[-1]).astype(jnp.float32)
    first_doc = (doc_index == 0).astype(jnp.float32)

    def mix(x_part, lo, hi):
        cum = cum_decay[:, lo:hi]
        step = step_size[:, lo:hi]
        cum_t = cum.T
        decay = jnp.exp(-jnp.abs(cum_t[:, :, None] - cum_t[:, None, :])) * same_doc[None]
        mixing = scores[None] * decay * step.T[:, None, :]
        x_heads = x_part.reshape(row_count, hi - lo, head_size).astype(jnp.float32)
        y_local = jnp.einsum("hts,shp->thp", mixing, x_heads, precision=HIGH)
        end_weight = jnp.exp(cum[-1][None, :] - cum) * last_doc[:, None] * step
        begin_weight = jnp.exp(cum) * first_doc[:, None] * step
        state_end = jnp.einsum("tn,th,thp->hnp", b_float, end_weight, x_heads, precision=HIGH)
        state_begin = jnp.einsum("tn,th,thp->hnp", b_float, begin_weight, x_heads, precision=HIGH)
        carry_gain = jnp.exp(cum[-1]) * (doc_index[-1] == 0)
        prefix = carried(carry_gain, state_end, "seq", False)
        suffix = carried(carry_gain, state_begin, "seq", True)
        left_gate = jnp.exp(cum) * first_doc[:, None]
        right_gate = jnp.exp(cum[-1][None, :] - cum) * last_doc[:, None]
        from_left = jnp.einsum("tn,hnp->thp", c_float, prefix, precision=HIGH)
        from_right = jnp.einsum("tn,hnp->thp", c_float, suffix, precision=HIGH)
        return (
            y_local
            + left_gate[:, :, None] * from_left
            + right_gate[:, :, None] * from_right
            + skip_gain[None, lo:hi, None] * x_heads
        )

    mixer = jnp.concatenate(
        [mix(x_parts[0], 0, split_heads), mix(x_parts[1], split_heads, head_count)], axis=1
    )
    mixer_rows = mixer.reshape(row_count, head_count * head_size)
    square_sum = lax.psum(jnp.sum(mixer_rows * mixer_rows, axis=1), "head")
    full_width = mixer_rows.shape[1] * lax.axis_size("head")
    inv_scale = lax.rsqrt(square_sum / full_width + 1e-05)
    return (mixer_rows * inv_scale[:, None] * norm_gain[None, :]).astype(jnp.bfloat16)[None]


def solution(mesh):
    placed = (
        P(("grp", "dp"), "seq", None),
        P(("grp", "dp"), "seq"),
        P(("grp", "dp"), "seq"),
        P(("seq", "dp"), "head"),
        P(("seq", "dp"), None),
        P(("seq", "dp"), "head"),
        P("head"),
        P("head"),
        P("head"),
        P("head"),
    )
    return jax.shard_map(
        per_device,
        mesh=mesh,
        in_specs=placed,
        out_specs=P(("grp", "dp"), "seq", "head"),
        check_vma=False,
    )
```

```python
import jax
import jax.numpy as jnp
from jax import lax
from jax.sharding import PartitionSpec as P

HIGH = lax.Precision.HIGHEST
CHUNKS = 4


def carried(gain, state, axis, reverse):
    count = lax.axis_size(axis)
    rows = state.shape[0] * state.shape[1]
    heads = gain.shape[0]
    pad = jnp.zeros((8, state.shape[2]), state.dtype).at[0, :heads].set(gain)
    value = jnp.concatenate([state.reshape(rows, -1), pad])
    total = jnp.zeros(state.shape, state.dtype)
    factor = jnp.ones((heads,), state.dtype)
    for step in range(1, count):
        if reverse:
            pairs = [(j, j - step) for j in range(step, count)]
        else:
            pairs = [(j, j + step) for j in range(count - step)]
        got = lax.ppermute(value, axis, pairs)
        total = total + factor[:, None, None] * got[:rows].reshape(state.shape)
        factor = factor * got[rows, :heads]
    return total


def per_device(
    tokens_in,
    positions,
    doc_start,
    feature_weight,
    state_weight,
    step_weight,
    step_bias,
    decay_log,
    skip_gain,
    norm_gain,
):
    row_count = tokens_in.shape[1]
    shards = lax.axis_size("seq")
    here = lax.axis_index("seq")
    slot = row_count // shards
    head_count = step_bias.shape[0]
    feat_cols = feature_weight.shape[1]
    head_size = feat_cols // head_count
    state_size = state_weight.shape[1] // 2

    seq_count = lax.axis_size("seq")
    dp_count = lax.axis_size("dp")
    block_rows = feature_weight.shape[0]
    parts = tokens_in[0].reshape(row_count, seq_count, dp_count, block_rows).transpose(2, 0, 1, 3)
    mine = lax.all_to_all(parts, "dp", 0, 0, tiled=True)
    mine = mine.reshape(dp_count * row_count, seq_count * block_rows)
    moved_positions = lax.all_to_all(
        positions[0].reshape(shards, slot), "seq", 0, 0, tiled=True
    ).reshape(row_count)
    offsets = moved_positions - here * row_count
    inverse = jnp.zeros((row_count,), jnp.int32).at[offsets].set(
        jnp.arange(row_count, dtype=jnp.int32)
    )

    def gather_rows(weights, offloaded):
        if offloaded:
            return lax.all_gather(weights, "seq", axis=0, tiled=True)
        spread = jnp.broadcast_to(weights[None], (seq_count,) + weights.shape)
        gathered = lax.all_to_all(spread, "seq", 0, 0, tiled=True)
        return gathered.reshape(seq_count * block_rows, -1)

    def project(gathered):
        partial = jnp.dot(mine, gathered, preferred_element_type=jnp.float32)
        projected = lax.psum_scatter(partial, "dp", scatter_dimension=0, tiled=True)
        projected = projected.astype(jnp.bfloat16).reshape(shards, slot, -1)
        moved = lax.all_to_all(projected, "seq", 0, 0, tiled=True).reshape(row_count, -1)
        return moved[inverse]

    group = head_count // CHUNKS
    width = group * head_size
    pieces = [jnp.concatenate([state_weight, step_weight, feature_weight[:, :width]], axis=1)]
    pieces += [feature_weight[:, k * width : (k + 1) * width] for k in range(1, CHUNKS)]
    gathered = gather_rows(pieces[0], True)
    outs = []
    for k in range(CHUNKS):
        if k + 1 < CHUNKS:
            following, gathered = lax.optimization_barrier((pieces[k + 1], gathered))
        outs.append(project(gathered))
        if k + 1 < CHUNKS:
            gathered = gather_rows(following, False)
    bc_proj = outs[0][:, : 2 * state_size]
    step_raw = outs[0][:, 2 * state_size : 2 * state_size + head_count]
    x_parts = [outs[0][:, 2 * state_size + head_count :]] + outs[1:]

    b_float = bc_proj[:, :state_size].astype(jnp.float32)
    c_float = bc_proj[:, state_size:].astype(jnp.float32)
    step_size = jax.nn.softplus(step_raw.astype(jnp.float32) + step_bias[None, :])
    log_decay = -jnp.exp(decay_log)[None, :] * step_size
    cum_decay = jnp.cumsum(log_decay, axis=0)
    doc_index = jnp.cumsum(doc_start[0], axis=0)
    scores = jnp.dot(
        bc_proj[:, state_size:], bc_proj[:, :state_size].T, preferred_element_type=jnp.float32
    )
    places = jnp.arange(row_count, dtype=jnp.int32)
    same_doc = (
        (doc_index[:, None] == doc_index[None, :]) & (places[:, None] != places[None, :])
    ).astype(jnp.float32)
    last_doc = (doc_index == doc_index[-1]).astype(jnp.float32)
    first_doc = (doc_index == 0).astype(jnp.float32)

    def mix(x_part, lo, hi):
        cum = cum_decay[:, lo:hi]
        step = step_size[:, lo:hi]
        cum_t = cum.T
        decay = jnp.exp(-jnp.abs(cum_t[:, :, None] - cum_t[:, None, :])) * same_doc[None]
        mixing = scores[None] * decay * step.T[:, None, :]
        x_heads = x_part.reshape(row_count, hi - lo, head_size).astype(jnp.float32)
        y_local = jnp.einsum("hts,shp->thp", mixing, x_heads, precision=HIGH)
        end_weight = jnp.exp(cum[-1][None, :] - cum) * last_doc[:, None] * step
        begin_weight = jnp.exp(cum) * first_doc[:, None] * step
        state_end = jnp.einsum("tn,th,thp->hnp", b_float, end_weight, x_heads, precision=HIGH)
        state_begin = jnp.einsum("tn,th,thp->hnp", b_float, begin_weight, x_heads, precision=HIGH)
        carry_gain = jnp.exp(cum[-1]) * (doc_index[-1] == 0)
        prefix = carried(carry_gain, state_end, "seq", False)
        suffix = carried(carry_gain, state_begin, "seq", True)
        left_gate = jnp.exp(cum) * first_doc[:, None]
        right_gate = jnp.exp(cum[-1][None, :] - cum) * last_doc[:, None]
        from_left = jnp.einsum("tn,hnp->thp", c_float, prefix, precision=HIGH)
        from_right = jnp.einsum("tn,hnp->thp", c_float, suffix, precision=HIGH)
        return (
            y_local
            + left_gate[:, :, None] * from_left
            + right_gate[:, :, None] * from_right
            + skip_gain[None, lo:hi, None] * x_heads
        )

    mixer = jnp.concatenate(
        [mix(x_parts[k], k * group, (k + 1) * group) for k in range(CHUNKS)], axis=1
    )
    mixer_rows = mixer.reshape(row_count, head_count * head_size)
    square_sum = lax.psum(jnp.sum(mixer_rows * mixer_rows, axis=1), "head")
    full_width = mixer_rows.shape[1] * lax.axis_size("head")
    inv_scale = lax.rsqrt(square_sum / full_width + 1e-05)
    return (mixer_rows * inv_scale[:, None] * norm_gain[None, :]).astype(jnp.bfloat16)[None]


def solution(mesh):
    placed = (
        P(("grp", "dp"), "seq", None),
        P(("grp", "dp"), "seq"),
        P(("grp", "dp"), "seq"),
        P(("seq", "dp"), "head"),
        P(("seq", "dp"), None),
        P(("seq", "dp"), "head"),
        P("head"),
        P("head"),
        P("head"),
        P("head"),
    )
    return jax.shard_map(
        per_device,
        mesh=mesh,
        in_specs=placed,
        out_specs=P(("grp", "dp"), "seq", "head"),
        check_vma=False,
    )
```

```python
import jax
import jax.numpy as jnp
from jax import lax
from jax.sharding import PartitionSpec as P

HIGH = lax.Precision.HIGHEST
CHUNKS = 2


def carried(gain, state_end, state_begin, axis):
    count = lax.axis_size(axis)
    here = lax.axis_index(axis)
    rows = state_end.shape[0] * state_end.shape[1]
    heads = gain.shape[0]
    pad = jnp.zeros((8, state_end.shape[2]), state_end.dtype).at[0, :heads].set(gain)
    ends = jnp.concatenate([state_end.reshape(rows, -1), pad])
    begins = jnp.concatenate([state_begin.reshape(rows, -1), pad])
    later = (jnp.arange(count) > here)[:, None, None]
    got = lax.all_to_all(jnp.where(later, ends[None], begins[None]), axis, 0, 0, tiled=True)
    gains = got[:, rows, :heads]
    states = got[:, :rows].reshape((count,) + state_end.shape)
    k = jnp.arange(count)[:, None]
    u = jnp.arange(count)[None, :]

    def weighted(between, source):
        factors = jnp.where(between[:, :, None], gains[None, :, :], 1.0)
        weight = jnp.prod(factors, axis=1) * source.astype(state_end.dtype)
        return jnp.sum(weight[:, :, None, None] * states, axis=0)

    prefix = weighted((u > k) & (u < here), k < here)
    suffix = weighted((u < k) & (u > here), k > here)
    return prefix, suffix


def per_device(
    tokens_in,
    positions,
    doc_start,
    feature_weight,
    state_weight,
    step_weight,
    step_bias,
    decay_log,
    skip_gain,
    norm_gain,
):
    row_count = tokens_in.shape[1]
    shards = lax.axis_size("seq")
    here = lax.axis_index("seq")
    slot = row_count // shards
    head_count = step_bias.shape[0]
    feat_cols = feature_weight.shape[1]
    head_size = feat_cols // head_count
    state_size = state_weight.shape[1] // 2

    seq_count = lax.axis_size("seq")
    dp_count = lax.axis_size("dp")
    block_rows = feature_weight.shape[0]
    parts = tokens_in[0].reshape(row_count, seq_count, dp_count, block_rows).transpose(2, 0, 1, 3)
    mine = lax.all_to_all(parts, "dp", 0, 0, tiled=True)
    mine = mine.reshape(dp_count * row_count, seq_count * block_rows)
    moved_positions = lax.all_to_all(
        positions[0].reshape(shards, slot), "seq", 0, 0, tiled=True
    ).reshape(row_count)
    offsets = moved_positions - here * row_count
    inverse = jnp.zeros((row_count,), jnp.int32).at[offsets].set(
        jnp.arange(row_count, dtype=jnp.int32)
    )

    def gather_rows(weights, offloaded):
        if offloaded:
            return lax.all_gather(weights, "seq", axis=0, tiled=True)
        spread = jnp.broadcast_to(weights[None], (seq_count,) + weights.shape)
        gathered = lax.all_to_all(spread, "seq", 0, 0, tiled=True)
        return gathered.reshape(seq_count * block_rows, -1)

    def project(gathered):
        partial = jnp.dot(mine, gathered, preferred_element_type=jnp.float32)
        projected = lax.psum_scatter(partial, "dp", scatter_dimension=0, tiled=True)
        projected = projected.astype(jnp.bfloat16).reshape(shards, slot, -1)
        moved = lax.all_to_all(projected, "seq", 0, 0, tiled=True).reshape(row_count, -1)
        return moved[inverse]

    group = head_count // CHUNKS
    width = group * head_size
    pieces = [jnp.concatenate([state_weight, step_weight, feature_weight[:, :width]], axis=1)]
    pieces += [feature_weight[:, k * width : (k + 1) * width] for k in range(1, CHUNKS)]
    gathered = gather_rows(pieces[0], True)
    outs = []
    for k in range(CHUNKS):
        if k + 1 < CHUNKS:
            following, gathered = lax.optimization_barrier((pieces[k + 1], gathered))
        outs.append(project(gathered))
        if k + 1 < CHUNKS:
            gathered = gather_rows(following, False)
    bc_proj = outs[0][:, : 2 * state_size]
    step_raw = outs[0][:, 2 * state_size : 2 * state_size + head_count]
    x_parts = [outs[0][:, 2 * state_size + head_count :]] + outs[1:]

    b_float = bc_proj[:, :state_size].astype(jnp.float32)
    c_float = bc_proj[:, state_size:].astype(jnp.float32)
    step_size = jax.nn.softplus(step_raw.astype(jnp.float32) + step_bias[None, :])
    log_decay = -jnp.exp(decay_log)[None, :] * step_size
    cum_decay = jnp.cumsum(log_decay, axis=0)
    doc_index = jnp.cumsum(doc_start[0], axis=0)
    scores = jnp.dot(
        bc_proj[:, state_size:], bc_proj[:, :state_size].T, preferred_element_type=jnp.float32
    )
    places = jnp.arange(row_count, dtype=jnp.int32)
    same_doc = (
        (doc_index[:, None] == doc_index[None, :]) & (places[:, None] != places[None, :])
    ).astype(jnp.float32)
    last_doc = (doc_index == doc_index[-1]).astype(jnp.float32)
    first_doc = (doc_index == 0).astype(jnp.float32)

    def mix(x_part, lo, hi):
        cum = cum_decay[:, lo:hi]
        step = step_size[:, lo:hi]
        cum_t = cum.T
        decay = jnp.exp(-jnp.abs(cum_t[:, :, None] - cum_t[:, None, :])) * same_doc[None]
        mixing = scores[None] * decay * step.T[:, None, :]
        x_heads = x_part.reshape(row_count, hi - lo, head_size).astype(jnp.float32)
        y_local = jnp.einsum("hts,shp->thp", mixing, x_heads, precision=HIGH)
        end_weight = jnp.exp(cum[-1][None, :] - cum) * last_doc[:, None] * step
        begin_weight = jnp.exp(cum) * first_doc[:, None] * step
        state_end = jnp.einsum("tn,th,thp->hnp", b_float, end_weight, x_heads, precision=HIGH)
        state_begin = jnp.einsum("tn,th,thp->hnp", b_float, begin_weight, x_heads, precision=HIGH)
        carry_gain = jnp.exp(cum[-1]) * (doc_index[-1] == 0)
        prefix, suffix = carried(carry_gain, state_end, state_begin, "seq")
        left_gate = jnp.exp(cum) * first_doc[:, None]
        right_gate = jnp.exp(cum[-1][None, :] - cum) * last_doc[:, None]
        from_left = jnp.einsum("tn,hnp->thp", c_float, prefix, precision=HIGH)
        from_right = jnp.einsum("tn,hnp->thp", c_float, suffix, precision=HIGH)
        return (
            y_local
            + left_gate[:, :, None] * from_left
            + right_gate[:, :, None] * from_right
            + skip_gain[None, lo:hi, None] * x_heads
        )

    mixer = jnp.concatenate(
        [mix(x_parts[k], k * group, (k + 1) * group) for k in range(CHUNKS)], axis=1
    )
    mixer_rows = mixer.reshape(row_count, head_count * head_size)
    square_sum = lax.psum(jnp.sum(mixer_rows * mixer_rows, axis=1), "head")
    full_width = mixer_rows.shape[1] * lax.axis_size("head")
    inv_scale = lax.rsqrt(square_sum / full_width + 1e-05)
    return (mixer_rows * inv_scale[:, None] * norm_gain[None, :]).astype(jnp.bfloat16)[None]


def solution(mesh):
    placed = (
        P(("grp", "dp"), "seq", None),
        P(("grp", "dp"), "seq"),
        P(("grp", "dp"), "seq"),
        P(("seq", "dp"), "head"),
        P(("seq", "dp"), None),
        P(("seq", "dp"), "head"),
        P("head"),
        P("head"),
        P("head"),
        P("head"),
    )
    return jax.shard_map(
        per_device,
        mesh=mesh,
        in_specs=placed,
        out_specs=P(("grp", "dp"), "seq", "head"),
        check_vma=False,
    )
```

```python
import jax
import jax.numpy as jnp
from jax import lax
from jax.sharding import PartitionSpec as P

HIGH = lax.Precision.HIGHEST


def carried(gain, state_end, state_begin, axis):
    count = lax.axis_size(axis)
    here = lax.axis_index(axis)
    rows = state_end.shape[0] * state_end.shape[1]
    heads = gain.shape[0]
    pad = jnp.zeros((8, state_end.shape[2]), state_end.dtype).at[0, :heads].set(gain)
    ends = jnp.concatenate([state_end.reshape(rows, -1), pad])
    begins = jnp.concatenate([state_begin.reshape(rows, -1), pad])
    got = []
    for step in range(1, count):
        pairs = [(j, (j + step) % count) for j in range(count)]
        got.append(lax.ppermute(jnp.where(here + step < count, ends, begins), axis, pairs))
    got = jnp.stack(got)
    source = (here - jnp.arange(1, count)) % count
    gains = got[:, rows, :heads]
    states = got[:, :rows].reshape((count - 1,) + state_end.shape)
    k = source[:, None]
    u = source[None, :]

    def weighted(between, chosen):
        factors = jnp.where(between[:, :, None], gains[None, :, :], 1.0)
        weight = jnp.prod(factors, axis=1) * chosen.astype(state_end.dtype)[:, None]
        return jnp.sum(weight[:, :, None, None] * states, axis=0)

    prefix = weighted((u > k) & (u < here), source < here)
    suffix = weighted((u < k) & (u > here), source > here)
    return prefix, suffix


def per_device(
    tokens_in,
    positions,
    doc_start,
    feature_weight,
    state_weight,
    step_weight,
    step_bias,
    decay_log,
    skip_gain,
    norm_gain,
):
    row_count = tokens_in.shape[1]
    shards = lax.axis_size("seq")
    here = lax.axis_index("seq")
    slot = row_count // shards
    head_count = step_bias.shape[0]
    feat_cols = feature_weight.shape[1]
    head_size = feat_cols // head_count
    state_size = state_weight.shape[1] // 2

    seq_count = lax.axis_size("seq")
    dp_count = lax.axis_size("dp")
    block_rows = feature_weight.shape[0]
    parts = tokens_in[0].reshape(row_count, seq_count, dp_count, block_rows).transpose(2, 0, 1, 3)
    mine = lax.all_to_all(parts, "dp", 0, 0, tiled=True)
    mine = mine.reshape(dp_count * row_count, seq_count * block_rows)
    moved_positions = lax.all_to_all(
        positions[0].reshape(shards, slot), "seq", 0, 0, tiled=True
    ).reshape(row_count)
    offsets = moved_positions - here * row_count
    inverse = jnp.zeros((row_count,), jnp.int32).at[offsets].set(
        jnp.arange(row_count, dtype=jnp.int32)
    )

    def gather_rows(weights, offloaded):
        if offloaded:
            return lax.all_gather(weights, "seq", axis=0, tiled=True)
        spread = jnp.broadcast_to(weights[None], (seq_count,) + weights.shape)
        gathered = lax.all_to_all(spread, "seq", 0, 0, tiled=True)
        return gathered.reshape(seq_count * block_rows, -1)

    def project(gathered):
        partial = jnp.dot(mine, gathered, preferred_element_type=jnp.float32)
        projected = lax.psum_scatter(partial, "dp", scatter_dimension=0, tiled=True)
        projected = projected.astype(jnp.bfloat16).reshape(shards, slot, -1)
        moved = lax.all_to_all(projected, "seq", 0, 0, tiled=True).reshape(row_count, -1)
        return moved[inverse]

    split_heads = head_count // 2
    split = split_heads * head_size
    gathered_first = gather_rows(
        jnp.concatenate([state_weight, step_weight, feature_weight[:, :split]], axis=1), True
    )
    rest, gathered_first = lax.optimization_barrier((feature_weight[:, split:], gathered_first))
    first = project(gathered_first)
    second = project(gather_rows(rest, False))
    bc_proj = first[:, : 2 * state_size]
    step_raw = first[:, 2 * state_size : 2 * state_size + head_count]
    x_parts = (first[:, 2 * state_size + head_count :], second)

    b_float = bc_proj[:, :state_size].astype(jnp.float32)
    c_float = bc_proj[:, state_size:].astype(jnp.float32)
    step_size = jax.nn.softplus(step_raw.astype(jnp.float32) + step_bias[None, :])
    log_decay = -jnp.exp(decay_log)[None, :] * step_size
    cum_decay = jnp.cumsum(log_decay, axis=0)
    doc_index = jnp.cumsum(doc_start[0], axis=0)
    scores = jnp.dot(
        bc_proj[:, state_size:], bc_proj[:, :state_size].T, preferred_element_type=jnp.float32
    )
    places = jnp.arange(row_count, dtype=jnp.int32)
    same_doc = (
        (doc_index[:, None] == doc_index[None, :]) & (places[:, None] != places[None, :])
    ).astype(jnp.float32)
    last_doc = (doc_index == doc_index[-1]).astype(jnp.float32)
    first_doc = (doc_index == 0).astype(jnp.float32)

    def mix(x_part, lo, hi):
        cum = cum_decay[:, lo:hi]
        step = step_size[:, lo:hi]
        cum_t = cum.T
        decay = jnp.exp(-jnp.abs(cum_t[:, :, None] - cum_t[:, None, :])) * same_doc[None]
        mixing = scores[None] * decay * step.T[:, None, :]
        x_heads = x_part.reshape(row_count, hi - lo, head_size).astype(jnp.float32)
        y_local = jnp.einsum("hts,shp->thp", mixing, x_heads, precision=HIGH)
        end_weight = jnp.exp(cum[-1][None, :] - cum) * last_doc[:, None] * step
        begin_weight = jnp.exp(cum) * first_doc[:, None] * step
        state_end = jnp.einsum("tn,th,thp->hnp", b_float, end_weight, x_heads, precision=HIGH)
        state_begin = jnp.einsum("tn,th,thp->hnp", b_float, begin_weight, x_heads, precision=HIGH)
        carry_gain = jnp.exp(cum[-1]) * (doc_index[-1] == 0)
        prefix, suffix = carried(carry_gain, state_end, state_begin, "seq")
        left_gate = jnp.exp(cum) * first_doc[:, None]
        right_gate = jnp.exp(cum[-1][None, :] - cum) * last_doc[:, None]
        from_left = jnp.einsum("tn,hnp->thp", c_float, prefix, precision=HIGH)
        from_right = jnp.einsum("tn,hnp->thp", c_float, suffix, precision=HIGH)
        return (
            y_local
            + left_gate[:, :, None] * from_left
            + right_gate[:, :, None] * from_right
            + skip_gain[None, lo:hi, None] * x_heads
        )

    mixer = jnp.concatenate(
        [mix(x_parts[0], 0, split_heads), mix(x_parts[1], split_heads, head_count)], axis=1
    )
    mixer_rows = mixer.reshape(row_count, head_count * head_size)
    square_sum = lax.psum(jnp.sum(mixer_rows * mixer_rows, axis=1), "head")
    full_width = mixer_rows.shape[1] * lax.axis_size("head")
    inv_scale = lax.rsqrt(square_sum / full_width + 1e-05)
    return (mixer_rows * inv_scale[:, None] * norm_gain[None, :]).astype(jnp.bfloat16)[None]


def solution(mesh):
    placed = (
        P(("grp", "dp"), "seq", None),
        P(("grp", "dp"), "seq"),
        P(("grp", "dp"), "seq"),
        P(("seq", "dp"), "head"),
        P(("seq", "dp"), None),
        P(("seq", "dp"), "head"),
        P("head"),
        P("head"),
        P("head"),
        P("head"),
    )
    return jax.shard_map(
        per_device,
        mesh=mesh,
        in_specs=placed,
        out_specs=P(("grp", "dp"), "seq", "head"),
        check_vma=False,
    )
```

```python
import jax
import jax.numpy as jnp
from jax import lax
from jax.sharding import PartitionSpec as P

HIGH = lax.Precision.HIGHEST


def carried(gain, state, axis, reverse):
    count = lax.axis_size(axis)
    rows = state.shape[0] * state.shape[1]
    heads = gain.shape[0]
    pad = jnp.zeros((8, state.shape[2]), state.dtype).at[0, :heads].set(gain)
    value = jnp.concatenate([state.reshape(rows, -1), pad])
    total = jnp.zeros(state.shape, state.dtype)
    factor = jnp.ones((heads,), state.dtype)
    for step in range(1, count):
        if reverse:
            pairs = [(j, j - step) for j in range(step, count)]
        else:
            pairs = [(j, j + step) for j in range(count - step)]
        got = lax.ppermute(value, axis, pairs)
        total = total + factor[:, None, None] * got[:rows].reshape(state.shape)
        factor = factor * got[rows, :heads]
    return total


def per_device(
    tokens_in,
    positions,
    doc_start,
    feature_weight,
    state_weight,
    step_weight,
    step_bias,
    decay_log,
    skip_gain,
    norm_gain,
):
    row_count = tokens_in.shape[1]
    shards = lax.axis_size("seq")
    here = lax.axis_index("seq")
    slot = row_count // shards
    head_count = step_bias.shape[0]
    feat_cols = feature_weight.shape[1]
    head_size = feat_cols // head_count
    state_size = state_weight.shape[1] // 2

    seq_count = lax.axis_size("seq")
    dp_count = lax.axis_size("dp")
    block_rows = feature_weight.shape[0]
    moved_positions = lax.all_to_all(
        positions[0].reshape(shards, slot), "seq", 0, 0, tiled=True
    ).reshape(row_count)
    offsets = moved_positions - here * row_count
    inverse = jnp.zeros((row_count,), jnp.int32).at[offsets].set(
        jnp.arange(row_count, dtype=jnp.int32)
    )

    inverse, tokens = lax.optimization_barrier((inverse, tokens_in[0]))
    parts = tokens.reshape(row_count, seq_count, dp_count, block_rows).transpose(2, 0, 1, 3)
    mine = lax.all_to_all(parts, "dp", 0, 0, tiled=True)
    mine = mine.reshape(dp_count * row_count, seq_count * block_rows)

    def gather_rows(weights, offloaded):
        if offloaded:
            return lax.all_gather(weights, "seq", axis=0, tiled=True)
        spread = jnp.broadcast_to(weights[None], (seq_count,) + weights.shape)
        gathered = lax.all_to_all(spread, "seq", 0, 0, tiled=True)
        return gathered.reshape(seq_count * block_rows, -1)

    def project(gathered):
        partial = jnp.dot(mine, gathered, preferred_element_type=jnp.float32)
        projected = lax.psum_scatter(partial, "dp", scatter_dimension=0, tiled=True)
        projected = projected.astype(jnp.bfloat16).reshape(shards, slot, -1)
        moved = lax.all_to_all(projected, "seq", 0, 0, tiled=True).reshape(row_count, -1)
        return moved[inverse]

    split_heads = head_count // 2
    split = split_heads * head_size
    gathered_first = gather_rows(
        jnp.concatenate([state_weight, step_weight, feature_weight[:, :split]], axis=1), True
    )
    rest, gathered_first = lax.optimization_barrier((feature_weight[:, split:], gathered_first))
    first = project(gathered_first)
    second = project(gather_rows(rest, False))
    bc_proj = first[:, : 2 * state_size]
    step_raw = first[:, 2 * state_size : 2 * state_size + head_count]
    x_parts = (first[:, 2 * state_size + head_count :], second)

    b_float = bc_proj[:, :state_size].astype(jnp.float32)
    c_float = bc_proj[:, state_size:].astype(jnp.float32)
    step_size = jax.nn.softplus(step_raw.astype(jnp.float32) + step_bias[None, :])
    log_decay = -jnp.exp(decay_log)[None, :] * step_size
    cum_decay = jnp.cumsum(log_decay, axis=0)
    doc_index = jnp.cumsum(doc_start[0], axis=0)
    scores = jnp.dot(
        bc_proj[:, state_size:], bc_proj[:, :state_size].T, preferred_element_type=jnp.float32
    )
    places = jnp.arange(row_count, dtype=jnp.int32)
    same_doc = (
        (doc_index[:, None] == doc_index[None, :]) & (places[:, None] != places[None, :])
    ).astype(jnp.float32)
    last_doc = (doc_index == doc_index[-1]).astype(jnp.float32)
    first_doc = (doc_index == 0).astype(jnp.float32)

    def mix(x_part, lo, hi):
        cum = cum_decay[:, lo:hi]
        step = step_size[:, lo:hi]
        cum_t = cum.T
        decay = jnp.exp(-jnp.abs(cum_t[:, :, None] - cum_t[:, None, :])) * same_doc[None]
        mixing = scores[None] * decay * step.T[:, None, :]
        x_heads = x_part.reshape(row_count, hi - lo, head_size).astype(jnp.float32)
        y_local = jnp.einsum("hts,shp->thp", mixing, x_heads, precision=HIGH)
        end_weight = jnp.exp(cum[-1][None, :] - cum) * last_doc[:, None] * step
        begin_weight = jnp.exp(cum) * first_doc[:, None] * step
        state_end = jnp.einsum("tn,th,thp->hnp", b_float, end_weight, x_heads, precision=HIGH)
        state_begin = jnp.einsum("tn,th,thp->hnp", b_float, begin_weight, x_heads, precision=HIGH)
        carry_gain = jnp.exp(cum[-1]) * (doc_index[-1] == 0)
        prefix = carried(carry_gain, state_end, "seq", False)
        suffix = carried(carry_gain, state_begin, "seq", True)
        left_gate = jnp.exp(cum) * first_doc[:, None]
        right_gate = jnp.exp(cum[-1][None, :] - cum) * last_doc[:, None]
        from_left = jnp.einsum("tn,hnp->thp", c_float, prefix, precision=HIGH)
        from_right = jnp.einsum("tn,hnp->thp", c_float, suffix, precision=HIGH)
        return (
            y_local
            + left_gate[:, :, None] * from_left
            + right_gate[:, :, None] * from_right
            + skip_gain[None, lo:hi, None] * x_heads
        )

    mixer = jnp.concatenate(
        [mix(x_parts[0], 0, split_heads), mix(x_parts[1], split_heads, head_count)], axis=1
    )
    mixer_rows = mixer.reshape(row_count, head_count * head_size)
    square_sum = lax.psum(jnp.sum(mixer_rows * mixer_rows, axis=1), "head")
    full_width = mixer_rows.shape[1] * lax.axis_size("head")
    inv_scale = lax.rsqrt(square_sum / full_width + 1e-05)
    return (mixer_rows * inv_scale[:, None] * norm_gain[None, :]).astype(jnp.bfloat16)[None]


def solution(mesh):
    placed = (
        P(("grp", "dp"), "seq", None),
        P(("grp", "dp"), "seq"),
        P(("grp", "dp"), "seq"),
        P(("seq", "dp"), "head"),
        P(("seq", "dp"), None),
        P(("seq", "dp"), "head"),
        P("head"),
        P("head"),
        P("head"),
        P("head"),
    )
    return jax.shard_map(
        per_device,
        mesh=mesh,
        in_specs=placed,
        out_specs=P(("grp", "dp"), "seq", "head"),
        check_vma=False,
    )
```

```python
import jax
import jax.numpy as jnp
from jax import lax
from jax.sharding import PartitionSpec as P

HIGH = lax.Precision.HIGHEST


def carried(gain, state, axis, reverse):
    count = lax.axis_size(axis)
    rows = state.shape[0] * state.shape[1]
    heads = gain.shape[0]
    pad = jnp.zeros((8, state.shape[2]), state.dtype).at[0, :heads].set(gain)
    value = jnp.concatenate([state.reshape(rows, -1), pad])
    total = jnp.zeros(state.shape, state.dtype)
    factor = jnp.ones((heads,), state.dtype)
    for step in range(1, count):
        if reverse:
            pairs = [(j, j - step) for j in range(step, count)]
        else:
            pairs = [(j, j + step) for j in range(count - step)]
        got = lax.ppermute(value, axis, pairs)
        total = total + factor[:, None, None] * got[:rows].reshape(state.shape)
        factor = factor * got[rows, :heads]
    return total


def carried_both(gain, state_end, state_begin, axis):
    count = lax.axis_size(axis)
    here = lax.axis_index(axis)
    rows = state_end.shape[0] * state_end.shape[1]
    heads = gain.shape[0]
    pad = jnp.zeros((8, state_end.shape[2]), state_end.dtype).at[0, :heads].set(gain)
    ends = jnp.concatenate([state_end.reshape(rows, -1), pad])
    begins = jnp.concatenate([state_begin.reshape(rows, -1), pad])
    got = []
    for step in range(1, count):
        pairs = [(j, (j + step) % count) for j in range(count)]
        got.append(lax.ppermute(jnp.where(here + step < count, ends, begins), axis, pairs))
    got = jnp.stack(got)
    source = (here - jnp.arange(1, count)) % count
    gains = got[:, rows, :heads]
    states = got[:, :rows].reshape((count - 1,) + state_end.shape)
    k = source[:, None]
    u = source[None, :]

    def weighted(between, chosen):
        factors = jnp.where(between[:, :, None], gains[None, :, :], 1.0)
        weight = jnp.prod(factors, axis=1) * chosen.astype(state_end.dtype)[:, None]
        return jnp.sum(weight[:, :, None, None] * states, axis=0)

    prefix = weighted((u > k) & (u < here), source < here)
    suffix = weighted((u < k) & (u > here), source > here)
    return prefix, suffix


def per_device(
    tokens_in,
    positions,
    doc_start,
    feature_weight,
    state_weight,
    step_weight,
    step_bias,
    decay_log,
    skip_gain,
    norm_gain,
):
    row_count = tokens_in.shape[1]
    shards = lax.axis_size("seq")
    here = lax.axis_index("seq")
    slot = row_count // shards
    head_count = step_bias.shape[0]
    feat_cols = feature_weight.shape[1]
    head_size = feat_cols // head_count
    state_size = state_weight.shape[1] // 2

    seq_count = lax.axis_size("seq")
    dp_count = lax.axis_size("dp")
    block_rows = feature_weight.shape[0]
    moved_positions = lax.all_to_all(
        positions[0].reshape(shards, slot), "seq", 0, 0, tiled=True
    ).reshape(row_count)
    offsets = moved_positions - here * row_count
    inverse = jnp.zeros((row_count,), jnp.int32).at[offsets].set(
        jnp.arange(row_count, dtype=jnp.int32)
    )

    inverse, tokens = lax.optimization_barrier((inverse, tokens_in[0]))
    parts = tokens.reshape(row_count, seq_count, dp_count, block_rows).transpose(2, 0, 1, 3)
    mine = lax.all_to_all(parts, "dp", 0, 0, tiled=True)
    mine = mine.reshape(dp_count * row_count, seq_count * block_rows)

    def gather_rows(weights, offloaded):
        if offloaded:
            return lax.all_gather(weights, "seq", axis=0, tiled=True)
        spread = jnp.broadcast_to(weights[None], (seq_count,) + weights.shape)
        gathered = lax.all_to_all(spread, "seq", 0, 0, tiled=True)
        return gathered.reshape(seq_count * block_rows, -1)

    def project(gathered):
        partial = jnp.dot(mine, gathered, preferred_element_type=jnp.float32)
        projected = lax.psum_scatter(partial, "dp", scatter_dimension=0, tiled=True)
        projected = projected.astype(jnp.bfloat16).reshape(shards, slot, -1)
        moved = lax.all_to_all(projected, "seq", 0, 0, tiled=True).reshape(row_count, -1)
        return moved[inverse]

    split_heads = head_count // 2
    split = split_heads * head_size
    gathered_first = gather_rows(
        jnp.concatenate([state_weight, step_weight, feature_weight[:, :split]], axis=1), True
    )
    rest, gathered_first = lax.optimization_barrier((feature_weight[:, split:], gathered_first))
    first = project(gathered_first)
    second = project(gather_rows(rest, False))
    bc_proj = first[:, : 2 * state_size]
    step_raw = first[:, 2 * state_size : 2 * state_size + head_count]
    x_parts = (first[:, 2 * state_size + head_count :], second)

    b_float = bc_proj[:, :state_size].astype(jnp.float32)
    c_float = bc_proj[:, state_size:].astype(jnp.float32)
    step_size = jax.nn.softplus(step_raw.astype(jnp.float32) + step_bias[None, :])
    log_decay = -jnp.exp(decay_log)[None, :] * step_size
    cum_decay = jnp.cumsum(log_decay, axis=0)
    doc_index = jnp.cumsum(doc_start[0], axis=0)
    scores = jnp.dot(
        bc_proj[:, state_size:], bc_proj[:, :state_size].T, preferred_element_type=jnp.float32
    )
    places = jnp.arange(row_count, dtype=jnp.int32)
    same_doc = (
        (doc_index[:, None] == doc_index[None, :]) & (places[:, None] != places[None, :])
    ).astype(jnp.float32)
    last_doc = (doc_index == doc_index[-1]).astype(jnp.float32)
    first_doc = (doc_index == 0).astype(jnp.float32)

    def mix(x_part, lo, hi, cyclic):
        cum = cum_decay[:, lo:hi]
        step = step_size[:, lo:hi]
        cum_t = cum.T
        decay = jnp.exp(-jnp.abs(cum_t[:, :, None] - cum_t[:, None, :])) * same_doc[None]
        mixing = scores[None] * decay * step.T[:, None, :]
        x_heads = x_part.reshape(row_count, hi - lo, head_size).astype(jnp.float32)
        y_local = jnp.einsum("hts,shp->thp", mixing, x_heads, precision=HIGH)
        end_weight = jnp.exp(cum[-1][None, :] - cum) * last_doc[:, None] * step
        begin_weight = jnp.exp(cum) * first_doc[:, None] * step
        state_end = jnp.einsum("tn,th,thp->hnp", b_float, end_weight, x_heads, precision=HIGH)
        state_begin = jnp.einsum("tn,th,thp->hnp", b_float, begin_weight, x_heads, precision=HIGH)
        carry_gain = jnp.exp(cum[-1]) * (doc_index[-1] == 0)
        if cyclic:
            prefix, suffix = carried_both(carry_gain, state_end, state_begin, "seq")
        else:
            prefix = carried(carry_gain, state_end, "seq", False)
            suffix = carried(carry_gain, state_begin, "seq", True)
        left_gate = jnp.exp(cum) * first_doc[:, None]
        right_gate = jnp.exp(cum[-1][None, :] - cum) * last_doc[:, None]
        from_left = jnp.einsum("tn,hnp->thp", c_float, prefix, precision=HIGH)
        from_right = jnp.einsum("tn,hnp->thp", c_float, suffix, precision=HIGH)
        return (
            y_local
            + left_gate[:, :, None] * from_left
            + right_gate[:, :, None] * from_right
            + skip_gain[None, lo:hi, None] * x_heads
        )

    mixer = jnp.concatenate(
        [mix(x_parts[0], 0, split_heads, False), mix(x_parts[1], split_heads, head_count, True)],
        axis=1,
    )
    mixer_rows = mixer.reshape(row_count, head_count * head_size)
    square_sum = lax.psum(jnp.sum(mixer_rows * mixer_rows, axis=1), "head")
    full_width = mixer_rows.shape[1] * lax.axis_size("head")
    inv_scale = lax.rsqrt(square_sum / full_width + 1e-05)
    return (mixer_rows * inv_scale[:, None] * norm_gain[None, :]).astype(jnp.bfloat16)[None]


def solution(mesh):
    placed = (
        P(("grp", "dp"), "seq", None),
        P(("grp", "dp"), "seq"),
        P(("grp", "dp"), "seq"),
        P(("seq", "dp"), "head"),
        P(("seq", "dp"), None),
        P(("seq", "dp"), "head"),
        P("head"),
        P("head"),
        P("head"),
        P("head"),
    )
    return jax.shard_map(
        per_device,
        mesh=mesh,
        in_specs=placed,
        out_specs=P(("grp", "dp"), "seq", "head"),
        check_vma=False,
    )
```

```python
import jax
import jax.numpy as jnp
from jax import lax
from jax.sharding import PartitionSpec as P

HIGH = lax.Precision.HIGHEST


def carried(gain, state, axis, reverse):
    count = lax.axis_size(axis)
    rows = state.shape[0] * state.shape[1]
    heads = gain.shape[0]
    pad = jnp.zeros((8, state.shape[2]), state.dtype).at[0, :heads].set(gain)
    value = jnp.concatenate([state.reshape(rows, -1), pad])
    total = jnp.zeros(state.shape, state.dtype)
    factor = jnp.ones((heads,), state.dtype)
    for step in range(1, count):
        if reverse:
            pairs = [(j, j - step) for j in range(step, count)]
        else:
            pairs = [(j, j + step) for j in range(count - step)]
        got = lax.ppermute(value, axis, pairs)
        total = total + factor[:, None, None] * got[:rows].reshape(state.shape)
        factor = factor * got[rows, :heads]
    return total


def carried_both(gain, state_end, state_begin, axis):
    count = lax.axis_size(axis)
    here = lax.axis_index(axis)
    rows = state_end.shape[0] * state_end.shape[1]
    heads = gain.shape[0]
    pad = jnp.zeros((8, state_end.shape[2]), state_end.dtype).at[0, :heads].set(gain)
    ends = jnp.concatenate([state_end.reshape(rows, -1), pad])
    begins = jnp.concatenate([state_begin.reshape(rows, -1), pad])
    got = []
    for step in range(1, count):
        pairs = [(j, (j + step) % count) for j in range(count)]
        got.append(lax.ppermute(jnp.where(here + step < count, ends, begins), axis, pairs))
    got = jnp.stack(got)
    source = (here - jnp.arange(1, count)) % count
    gains = got[:, rows, :heads]
    states = got[:, :rows].reshape((count - 1,) + state_end.shape)
    k = source[:, None]
    u = source[None, :]

    def weighted(between, chosen):
        factors = jnp.where(between[:, :, None], gains[None, :, :], 1.0)
        weight = jnp.prod(factors, axis=1) * chosen.astype(state_end.dtype)[:, None]
        return jnp.sum(weight[:, :, None, None] * states, axis=0)

    prefix = weighted((u > k) & (u < here), source < here)
    suffix = weighted((u < k) & (u > here), source > here)
    return prefix, suffix


def per_device(
    tokens_in,
    positions,
    doc_start,
    feature_weight,
    state_weight,
    step_weight,
    step_bias,
    decay_log,
    skip_gain,
    norm_gain,
):
    row_count = tokens_in.shape[1]
    shards = lax.axis_size("seq")
    here = lax.axis_index("seq")
    slot = row_count // shards
    head_count = step_bias.shape[0]
    feat_cols = feature_weight.shape[1]
    head_size = feat_cols // head_count
    state_size = state_weight.shape[1] // 2

    seq_count = lax.axis_size("seq")
    dp_count = lax.axis_size("dp")
    block_rows = feature_weight.shape[0]
    moved_positions = lax.all_to_all(
        positions[0].reshape(shards, slot), "seq", 0, 0, tiled=True
    ).reshape(row_count)
    offsets = moved_positions - here * row_count
    inverse = jnp.zeros((row_count,), jnp.int32).at[offsets].set(
        jnp.arange(row_count, dtype=jnp.int32)
    )

    inverse, tokens = lax.optimization_barrier((inverse, tokens_in[0]))
    parts = tokens.reshape(row_count, seq_count, dp_count, block_rows).transpose(2, 0, 1, 3)
    mine = lax.all_to_all(parts, "dp", 0, 0, tiled=True)
    mine = mine.reshape(dp_count * row_count, seq_count * block_rows)

    def gather_rows(weights, offloaded):
        if offloaded:
            return lax.all_gather(weights, "seq", axis=0, tiled=True)
        spread = jnp.broadcast_to(weights[None], (seq_count,) + weights.shape)
        gathered = lax.all_to_all(spread, "seq", 0, 0, tiled=True)
        return gathered.reshape(seq_count * block_rows, -1)

    def project(gathered):
        partial = jnp.dot(mine, gathered, preferred_element_type=jnp.float32)
        projected = lax.psum_scatter(partial, "dp", scatter_dimension=0, tiled=True)
        projected = projected.astype(jnp.bfloat16).reshape(shards, slot, -1)
        moved = lax.all_to_all(projected, "seq", 0, 0, tiled=True).reshape(row_count, -1)
        return moved[inverse]

    split_heads = head_count // 2
    split = split_heads * head_size
    gathered_first = gather_rows(
        jnp.concatenate([state_weight, step_weight, feature_weight[:, :split]], axis=1), True
    )
    rest, gathered_first = lax.optimization_barrier((feature_weight[:, split:], gathered_first))
    first = project(gathered_first)
    second = project(gather_rows(rest, False))
    bc_proj = first[:, : 2 * state_size]
    step_raw = first[:, 2 * state_size : 2 * state_size + head_count]
    x_parts = (first[:, 2 * state_size + head_count :], second)

    b_float = bc_proj[:, :state_size].astype(jnp.float32)
    c_float = bc_proj[:, state_size:].astype(jnp.float32)
    step_size = jax.nn.softplus(step_raw.astype(jnp.float32) + step_bias[None, :])
    log_decay = -jnp.exp(decay_log)[None, :] * step_size
    cum_decay = jnp.cumsum(log_decay, axis=0)
    doc_index = jnp.cumsum(doc_start[0], axis=0)
    scores = jnp.dot(
        bc_proj[:, state_size:], bc_proj[:, :state_size].T, preferred_element_type=jnp.float32
    )
    places = jnp.arange(row_count, dtype=jnp.int32)
    same_doc = (
        (doc_index[:, None] == doc_index[None, :]) & (places[:, None] != places[None, :])
    ).astype(jnp.float32)
    last_doc = (doc_index == doc_index[-1]).astype(jnp.float32)
    first_doc = (doc_index == 0).astype(jnp.float32)

    def mix(x_part, lo, hi, cyclic):
        cum = cum_decay[:, lo:hi]
        step = step_size[:, lo:hi]
        cum_t = cum.T
        decay = jnp.exp(-jnp.abs(cum_t[:, :, None] - cum_t[:, None, :])) * same_doc[None]
        mixing = scores[None] * decay * step.T[:, None, :]
        x_heads = x_part.reshape(row_count, hi - lo, head_size).astype(jnp.float32)
        y_local = jnp.einsum("hts,shp->thp", mixing, x_heads, precision=HIGH)
        end_weight = jnp.exp(cum[-1][None, :] - cum) * last_doc[:, None] * step
        begin_weight = jnp.exp(cum) * first_doc[:, None] * step
        state_end = jnp.einsum("tn,th,thp->hnp", b_float, end_weight, x_heads, precision=HIGH)
        state_begin = jnp.einsum("tn,th,thp->hnp", b_float, begin_weight, x_heads, precision=HIGH)
        carry_gain = jnp.exp(cum[-1]) * (doc_index[-1] == 0)
        if cyclic:
            prefix, suffix = carried_both(carry_gain, state_end, state_begin, "seq")
        else:
            prefix = carried(carry_gain, state_end, "seq", False)
            suffix = carried(carry_gain, state_begin, "seq", True)
        left_gate = jnp.exp(cum) * first_doc[:, None]
        right_gate = jnp.exp(cum[-1][None, :] - cum) * last_doc[:, None]
        from_left = jnp.einsum("tn,hnp->thp", c_float, prefix, precision=HIGH)
        from_right = jnp.einsum("tn,hnp->thp", c_float, suffix, precision=HIGH)
        return (
            y_local
            + left_gate[:, :, None] * from_left
            + right_gate[:, :, None] * from_right
            + skip_gain[None, lo:hi, None] * x_heads
        )

    mixers = [
        mix(x_parts[0], 0, split_heads, False).reshape(row_count, split),
        mix(x_parts[1], split_heads, head_count, True).reshape(row_count, feat_cols - split),
    ]
    square_sum = lax.psum(sum(jnp.sum(m * m, axis=1) for m in mixers), "head")
    full_width = feat_cols * lax.axis_size("head")
    inv_scale = lax.rsqrt(square_sum / full_width + 1e-05)
    gains = (norm_gain[:split], norm_gain[split:])
    return jnp.concatenate(
        [(m * inv_scale[:, None] * g[None, :]).astype(jnp.bfloat16) for m, g in zip(mixers, gains)],
        axis=1,
    )[None]


def solution(mesh):
    placed = (
        P(("grp", "dp"), "seq", None),
        P(("grp", "dp"), "seq"),
        P(("grp", "dp"), "seq"),
        P(("seq", "dp"), "head"),
        P(("seq", "dp"), None),
        P(("seq", "dp"), "head"),
        P("head"),
        P("head"),
        P("head"),
        P("head"),
    )
    return jax.shard_map(
        per_device,
        mesh=mesh,
        in_specs=placed,
        out_specs=P(("grp", "dp"), "seq", "head"),
        check_vma=False,
    )
```
